512 devices in a mesh: ctx: 64 (over y, x, core), head: 8 (over z).
Axes of the slice: x: 4, y: 8, z: 8, core: 2. Of those that a mesh axis runs over, the one named last changes fastest.
Arguments:
- queries: bfloat16 [65536, 4096], P('ctx', 'head')
- keys: bfloat16 [65536, 4096], P('ctx', 'head'), may hold values from -5 to 5
- values: bfloat16 [65536, 4096], P('ctx', 'head')
- log_decay: float32 [65536, 32], P('ctx', 'head'), as said below
- gate: bfloat16 [65536, 4096], P('ctx', 'head'), may hold values from -6 to 6
- norm_gain: float32 [4096], replicated, may hold values from 0.1 to 1.9
Outputs:
- output: bfloat16 [65536, 4096], P(('ctx', 'head'))
The draws below stay inside these ranges and needn't reach their ends.
Inputs may be any that keep to these rules, and one draw needn't show every extreme that they name: `log_decay`: every entry is at most 0.
All inputs are finite; a program needn't handle non-finite values.
Results may differ from the reference program's by a relative error of at most 0.0085.
Values may be sent and summed in bfloat16 or wider, within the bound.
No kernel may reach another device: no remote copies, remote signals or barrier semaphores. Data moves between devices by JAX's collectives and lax.ppermute only.
A program may use at most 128 MiB of HBM per device.

```python
import math
import jax
import jax.numpy as jnp
from jax import lax

H = 32
HD = 128
TOK_DEV = 1024
HW = 4096
TOKENS = 65536


def draw_queries(key, part):
    first, second = jax.random.split(key)
    base = jnp.clip(jax.random.normal(first, (TOKENS, H, HD), jnp.float32), -4.0, 4.0)
    rows = jnp.exp(jax.random.uniform(second, (TOKENS, H, 1), jnp.float32, 0.0, math.log(10.0)))
    scaled = base * rows * (1.0 / math.sqrt(HD))
    return scaled.reshape(TOKENS, H * HD).astype(jnp.bfloat16)


def draw_values(key, part):
    column = jnp.arange(H * HD) // HD
    level = column.astype(jnp.float32) / (H - 1)
    base = jnp.clip(jax.random.normal(key, (TOKENS, H * HD), jnp.float32), -4.0, 4.0)
    scale = jnp.exp(level * math.log(10.0))
    return (base * scale[None, :]).astype(jnp.bfloat16)


def draw_log_decay(key, part):
    keys = jax.random.split(key, 7)
    order = jax.random.permutation(keys[0], H)
    fast_count = H // 2
    fast = order < fast_count
    slow_rate = jnp.exp(jax.random.uniform(keys[1], (H,), jnp.float32, math.log(0.03), math.log(0.3))) / TOKENS
    fast_rate = jnp.exp(jax.random.uniform(keys[2], (H,), jnp.float32, math.log(1.0 / 50.0), math.log(1.0 / 30.0)))
    forgetting_speed = jnp.where(fast, fast_rate, slow_rate)
    blocks = TOKENS // TOK_DEV
    segment_scaling_factor = jnp.exp(jax.random.uniform(keys[3], (blocks, 1, H), jnp.float32, -math.log(2.0), math.log(2.0)))
    segment_scaling_factor = jnp.broadcast_to(segment_scaling_factor, (blocks, TOK_DEV, H)).reshape(TOKENS, H)
    approximate_guess = jnp.exp(jax.random.uniform(keys[4], (TOKENS, H), jnp.float32, -0.33, 0.33))
    sample_indices = jax.random.randint(keys[5], (2, H), 0, TOKENS)
    objective_entries = jax.random.uniform(keys[6], (2, H), jnp.float32, math.log(0.5), math.log(0.8))
    target_index = jnp.arange(TOKENS)
    segment_partition = jnp.where(target_index[:, None] == sample_indices[0][None, :], objective_entries[0][None, :], 0.0)
    segment_partition = segment_partition + jnp.where(target_index[:, None] == sample_indices[1][None, :], objective_entries[1][None, :], 0.0)
    return (segment_partition - forgetting_speed[None, :] * segment_scaling_factor * approximate_guess).astype(jnp.float32)


def shard_levels(stream_key, shape, cuts, least, top_value):
    loudness, own = 1.0, jax.random.fold_in(stream_key, 6)
    for axis_at, blocks in cuts:
        steps = jnp.exp(jax.random.uniform(jax.random.fold_in(own, axis_at), (blocks,), jnp.float32, least / len(cuts), top_value / len(cuts)))
        loudness = loudness * jnp.repeat(steps, shape[axis_at] // blocks).reshape([-1 if axis == axis_at else 1 for axis in range(len(shape))])
    return loudness


def noise(rng, shape, width, limit, shards=(), held_as=jnp.bfloat16):
    values = jax.random.normal(rng, shape, jnp.float32) * width
    if len(shards) > 0:
        values = shard_levels(rng, shape, shards, -0.22, 0.18) * values
    return jnp.clip(values, min=-limit, max=limit).astype(held_as)


def setup_inputs(seed: int = 0) -> dict:
    seeds = jax.random.split(jax.random.key(seed), 7)
    queries = draw_queries(jax.random.fold_in(seeds[6], 71), 0)
    keys = noise(seeds[1], (TOKENS, HW), 1.0, 5.0, ((0, 64), (1, 8)))
    values = draw_values(jax.random.fold_in(seeds[6], 71), 0)
    log_decay = draw_log_decay(jax.random.fold_in(seeds[6], 71), 0)
    gate = noise(seeds[4], (TOKENS, HW), 1.5, 6.0, ((0, 64), (1, 8)))
    norm_gain = jnp.clip(1.0 + 0.18 * jax.random.normal(seeds[5], (HW,), jnp.float32), 0.1, 1.9)
    return dict(queries=queries, keys=keys, values=values, log_decay=log_decay, gate=gate, norm_gain=norm_gain)


eps_norm = 1e-05

def head_block(qh, kh, vh, ch):
    count = qh.shape[0]
    target_index = jnp.arange(count)
    causal = target_index[:, None] >= target_index[None, :]
    scores = jnp.dot(qh, kh.T, preferred_element_type=jnp.float32)
    spread = jnp.where(causal, ch[:, None] - ch[None, :], 0.0)
    weights = (scores * jnp.where(causal, jnp.exp(spread), 0.0)).astype(jnp.bfloat16)
    inner = jnp.dot(weights, vh, preferred_element_type=jnp.float32)
    keyed = kh.astype(jnp.float32) * jnp.exp(ch[-1] - ch)[:, None]
    state = jnp.dot(keyed.T, vh.astype(jnp.float32), precision=lax.Precision.HIGHEST)
    return (inner, state)

def split_heads(block, heads):
    count = block.shape[0]
    return block.reshape(count, heads, block.shape[1] // heads).transpose(1, 0, 2)

def local_block(queries, keys, values, log_decay):
    heads = log_decay.shape[1]
    cum = jnp.cumsum(log_decay, axis=0)
    inner, state = lax.map(lambda parts: head_block(parts[0], parts[1], parts[2], parts[3]), (split_heads(queries, heads), split_heads(keys, heads), split_heads(values, heads), cum.T))
    return (cum, inner, state)

def join_block(queries, cum, inner, carried):
    heads = cum.shape[1]
    count = queries.shape[0]
    qfloat = split_heads(queries, heads).astype(jnp.float32)
    across = jnp.einsum('hcd,hde->hce', qfloat, carried, precision=lax.Precision.HIGHEST)
    total = inner + jnp.exp(cum).T[:, :, None] * across
    return total.transpose(1, 0, 2).reshape(count, queries.shape[1]).astype(jnp.bfloat16)

def normalize(attended, gate, gain):
    shade = attended.astype(jnp.float32)
    scale = lax.rsqrt(lax.optimization_barrier(jnp.mean(shade * shade, axis=1, keepdims=True)) + eps_norm)
    return (shade * scale * gain * jax.nn.sigmoid(gate.astype(jnp.float32))).astype(jnp.bfloat16)

def reference(queries, keys, values, log_decay, gate, norm_gain):
    blocks = TOKENS // TOK_DEV

    def reshaped(array):
        return array.reshape(blocks, TOK_DEV, array.shape[1])

    def advance(carried, pieces):
        qblock, kblock, vblock, dblock = pieces
        cum, inner, state = local_block(qblock, kblock, vblock, dblock)
        attended = join_block(qblock, cum, inner, carried)
        carried = jnp.exp(cum[-1])[:, None, None] * carried + state
        return (carried, attended)
    start_state = jnp.zeros((H, HD, HD), jnp.float32)
    final_state, attended = lax.scan(advance, start_state, (reshaped(queries), reshaped(keys), reshaped(values), reshaped(log_decay)))
    attended = attended.reshape(TOKENS, H * HD)
    return normalize(attended, gate, norm_gain)
```

```python
import jax
import jax.numpy as jnp
from jax import lax
from jax.sharding import Mesh, PartitionSpec as P

eps_norm = 1e-05
HI = lax.Precision.HIGHEST
F32 = jnp.float32


def split_ctx(mesh):
    devices = mesh.devices
    ctx_devices = list(devices[:, 0])
    rows = len({d.coords[1] for d in ctx_devices})
    cols = len({d.coords[0] for d in ctx_devices})
    cores = len(ctx_devices) // (rows * cols)
    shape = (rows, cols, cores, devices.shape[1])
    return Mesh(devices.reshape(shape), ("cy", "cx", "cc", "head"))


def shifted(x, axis, n):
    out = [x]
    for s in range(1, n):
        out.append(lax.ppermute(x, axis, [(j, (j + s) % n) for j in range(n)]))
    return out


def scan_pieces(logs, states, i, n):
    log_before = jnp.zeros_like(logs[0])
    before = jnp.zeros_like(states[0])
    log_after = jnp.zeros_like(logs[0])
    after = jnp.zeros_like(states[0])
    for s in range(1, n):
        early = s <= i
        weight_b = jnp.where(early, jnp.exp(log_before), 0.0)
        weight_a = jnp.where(early, 0.0, jnp.exp(log_after))
        before = before + weight_b[:, None, None] * states[s]
        after = after + weight_a[:, None, None] * states[s]
        log_before = log_before + jnp.where(early, logs[s], 0.0)
        log_after = log_after + jnp.where(early, 0.0, logs[s])
    return log_before, before, log_after, after


def carried_state(L, S):
    rows, cols, cores = lax.axis_size("cy"), lax.axis_size("cx"), lax.axis_size("cc")
    y, x, c = lax.axis_index("cy"), lax.axis_index("cx"), lax.axis_index("cc")
    heads, size = S.shape[0], S.shape[1]
    group = heads // cores

    pair = lax.ppermute((L, S), "cc", [(0, 1), (1, 0)])
    L0 = jnp.where(c == 0, L, pair[0])
    S0 = jnp.where(c == 0, S, pair[1])
    L1 = jnp.where(c == 0, pair[0], L)
    S1 = jnp.where(c == 0, pair[1], S)
    chip_log = L0 + L1
    chip_state = jnp.exp(L1)[:, None, None] * S0 + S1
    g_log = lax.dynamic_slice_in_dim(chip_log, c * group, group, 0)
    g_state = lax.dynamic_slice_in_dim(chip_state, c * group, group, 0)

    row_pieces = shifted((g_log, g_state), "cx", cols)
    e_log, e_state, f_log, f_state = scan_pieces(
        [p[0] for p in row_pieces], [p[1] for p in row_pieces], x, cols
    )
    row_log = e_log + g_log + f_log
    row_state = jnp.exp(f_log)[:, None, None] * (jnp.exp(g_log)[:, None, None] * e_state + g_state) + f_state

    part = size // cols
    q_state = lax.dynamic_slice_in_dim(row_state, x * part, part, 1)
    col_pieces = shifted((row_log, q_state), "cy", rows)
    y_log, y_state, _, _ = scan_pieces([p[0] for p in col_pieces], [p[1] for p in col_pieces], y, rows)

    parts = shifted(y_state, "cx", cols)
    ordered = [lax.select_n((x - q) % cols, *parts) for q in range(cols)]
    y_full = jnp.concatenate(ordered, axis=1)

    chip_before = jnp.exp(e_log)[:, None, None] * y_full + e_state

    other = lax.ppermute(chip_before, "cc", [(0, 1), (1, 0)])
    full0 = jnp.concatenate([chip_before, other], axis=0)
    full1 = jnp.concatenate([other, chip_before], axis=0)
    chip_full = jnp.where(c == 0, full0, full1)
    return jnp.where(c == 0, chip_full, jnp.exp(L0)[:, None, None] * chip_full + S0)


def inner_head(qh, kh, vh, ch):
    count = qh.shape[0]
    target_index = jnp.arange(count)
    causal = target_index[:, None] >= target_index[None, :]
    scores = jnp.dot(qh, kh.T, preferred_element_type=F32)
    spread = jnp.where(causal, ch[:, None] - ch[None, :], 0.0)
    weights = (scores * jnp.where(causal, jnp.exp(spread), 0.0)).astype(jnp.bfloat16)
    return jnp.dot(weights, vh, preferred_element_type=F32)


def body(queries, keys, values, log_decay, gate, norm_gain):
    count, width = queries.shape
    heads = log_decay.shape[1]
    size = width // heads
    cum = jnp.cumsum(log_decay, axis=0)
    last = cum[-1]

    k3 = keys.reshape(count, heads, size)
    v3 = values.reshape(count, heads, size)
    q3 = queries.reshape(count, heads, size)
    keyed = k3.astype(F32) * jnp.exp(last[None, :] - cum)[:, :, None]
    state = jnp.einsum("thd,the->hde", keyed, v3.astype(F32), precision=HI)

    carried = carried_state(last, state)

    inner = jnp.stack(
        [inner_head(q3[:, h], k3[:, h], v3[:, h], cum[:, h]) for h in range(heads)], axis=1
    )
    across = jnp.einsum("thd,hde->the", q3.astype(F32), carried, precision=HI)
    attended = (inner + jnp.exp(cum)[:, :, None] * across).reshape(count, width).astype(jnp.bfloat16)

    shade = attended.astype(F32)
    sums = lax.psum(jnp.sum(shade * shade, axis=1), "head")
    columns = width * lax.axis_size("head")
    scale = lax.rsqrt(sums / columns + eps_norm)[:, None]
    gain = lax.dynamic_slice_in_dim(norm_gain, lax.axis_index("head") * width, width, 0)
    shaped = (shade * scale * gain * jax.nn.sigmoid(gate.astype(F32))).astype(jnp.bfloat16)
    return lax.all_to_all(shaped, "head", split_axis=0, concat_axis=1, tiled=True)


def solution(mesh):
    fine = split_ctx(mesh)
    ctx = ("cy", "cx", "cc")
    spec = P(ctx, "head")
    in_specs = (spec, spec, spec, spec, spec, P())
    out_specs = P((*ctx, "head"), None)
    return jax.shard_map(body, mesh=fine, in_specs=in_specs, out_specs=out_specs, check_vma=False)
```

```python
import jax
import jax.numpy as jnp
from jax import lax
from jax.sharding import Mesh, PartitionSpec as P

eps_norm = 1e-05
HI = lax.Precision.HIGHEST
F32 = jnp.float32


def split_ctx(mesh):
    devices = mesh.devices
    ctx_devices = list(devices[:, 0])
    rows = len({d.coords[1] for d in ctx_devices})
    cols = len({d.coords[0] for d in ctx_devices})
    cores = len(ctx_devices) // (rows * cols)
    shape = (rows, cols, cores, devices.shape[1])
    return Mesh(devices.reshape(shape), ("cy", "cx", "cc", "head"))


def pack(log, state):
    row = jnp.broadcast_to(log[:, None, None], (state.shape[0], 1, state.shape[2]))
    return jnp.concatenate([state, row], axis=1)


def unpack(packed):
    return packed[:, -1, 0], packed[:, :-1]


def shifted(x, axis, n):
    out = [x]
    for s in range(1, n):
        out.append(lax.ppermute(x, axis, [(j, (j + s) % n) for j in range(n)]))
    return out


def scan_pieces(logs, states, i, n):
    log_before = jnp.zeros_like(logs[0])
    before = jnp.zeros_like(states[0])
    log_after = jnp.zeros_like(logs[0])
    after = jnp.zeros_like(states[0])
    for s in range(1, n):
        early = s <= i
        weight_b = jnp.where(early, jnp.exp(log_before), 0.0)
        weight_a = jnp.where(early, 0.0, jnp.exp(log_after))
        before = before + weight_b[:, None, None] * states[s]
        after = after + weight_a[:, None, None] * states[s]
        log_before = log_before + jnp.where(early, logs[s], 0.0)
        log_after = log_after + jnp.where(early, 0.0, logs[s])
    return log_before, before, log_after, after


def carried_state(L, S):
    rows, cols, cores = lax.axis_size("cy"), lax.axis_size("cx"), lax.axis_size("cc")
    y, x, c = lax.axis_index("cy"), lax.axis_index("cx"), lax.axis_index("cc")
    heads, size = S.shape[0], S.shape[1]
    group = heads // cores

    pair = unpack(lax.ppermute(pack(L, S), "cc", [(0, 1), (1, 0)]))
    L0 = jnp.where(c == 0, L, pair[0])
    S0 = jnp.where(c == 0, S, pair[1])
    L1 = jnp.where(c == 0, pair[0], L)
    S1 = jnp.where(c == 0, pair[1], S)
    chip_log = L0 + L1
    chip_state = jnp.exp(L1)[:, None, None] * S0 + S1
    g_log = lax.dynamic_slice_in_dim(chip_log, c * group, group, 0)
    g_state = lax.dynamic_slice_in_dim(chip_state, c * group, group, 0)

    row_pieces = [unpack(p) for p in shifted(pack(g_log, g_state), "cx", cols)]
    e_log, e_state, f_log, f_state = scan_pieces(
        [p[0] for p in row_pieces], [p[1] for p in row_pieces], x, cols
    )
    row_log = e_log + g_log + f_log
    row_state = jnp.exp(f_log)[:, None, None] * (jnp.exp(g_log)[:, None, None] * e_state + g_state) + f_state

    part = size // cols
    q_state = lax.dynamic_slice_in_dim(row_state, x * part, part, 1)
    col_pieces = [unpack(p) for p in shifted(pack(row_log, q_state), "cy", rows)]
    y_log, y_state, _, _ = scan_pieces([p[0] for p in col_pieces], [p[1] for p in col_pieces], y, rows)

    parts = shifted(y_state, "cx", cols)
    ordered = [lax.select_n((x - q) % cols, *parts) for q in range(cols)]
    y_full = jnp.concatenate(ordered, axis=1)

    chip_before = jnp.exp(e_log)[:, None, None] * y_full + e_state

    other = lax.ppermute(chip_before, "cc", [(0, 1), (1, 0)])
    full0 = jnp.concatenate([chip_before, other], axis=0)
    full1 = jnp.concatenate([other, chip_before], axis=0)
    chip_full = jnp.where(c == 0, full0, full1)
    return jnp.where(c == 0, chip_full, jnp.exp(L0)[:, None, None] * chip_full + S0)


def inner_head(qh, kh, vh, ch):
    count = qh.shape[0]
    target_index = jnp.arange(count)
    causal = target_index[:, None] >= target_index[None, :]
    scores = jnp.dot(qh, kh.T, preferred_element_type=F32)
    spread = jnp.where(causal, ch[:, None] - ch[None, :], 0.0)
    weights = (scores * jnp.where(causal, jnp.exp(spread), 0.0)).astype(jnp.bfloat16)
    return jnp.dot(weights, vh, preferred_element_type=F32)


def body(queries, keys, values, log_decay, gate, norm_gain):
    count, width = queries.shape
    heads = log_decay.shape[1]
    size = width // heads
    cum = jnp.cumsum(log_decay, axis=0)
    last = cum[-1]

    k3 = keys.reshape(count, heads, size)
    v3 = values.reshape(count, heads, size)
    q3 = queries.reshape(count, heads, size)
    keyed = k3.astype(F32) * jnp.exp(last[None, :] - cum)[:, :, None]
    state = jnp.einsum("thd,the->hde", keyed, v3.astype(F32), precision=HI)

    carried = carried_state(last, state)

    inner = jnp.stack(
        [inner_head(q3[:, h], k3[:, h], v3[:, h], cum[:, h]) for h in range(heads)], axis=1
    )
    across = jnp.einsum("thd,hde->the", q3.astype(F32), carried, precision=HI)
    attended = (inner + jnp.exp(cum)[:, :, None] * across).reshape(count, width).astype(jnp.bfloat16)

    groups = lax.axis_size("head")
    shade = attended.astype(F32)
    sums = jnp.sum(shade * shade, axis=1)
    gain = lax.dynamic_slice_in_dim(norm_gain, lax.axis_index("head") * width, width, 0)
    shaped = (shade * gain * jax.nn.sigmoid(gate.astype(F32))).astype(jnp.bfloat16)
    chunk = count // groups
    high = sums.astype(jnp.bfloat16)
    low = (sums - high.astype(F32)).astype(jnp.bfloat16)
    extra = jnp.zeros((groups, 1, width), jnp.bfloat16)
    extra = extra.at[:, 0, :chunk].set(high.reshape(groups, chunk))
    extra = extra.at[:, 0, chunk : 2 * chunk].set(low.reshape(groups, chunk))
    payload = jnp.concatenate([shaped.reshape(groups, chunk, width), extra], axis=1)
    got = lax.all_to_all(payload, "head", split_axis=0, concat_axis=0, tiled=True)
    parts = got[:, -1, :].astype(F32)
    total = jnp.sum(parts[:, :chunk] + parts[:, chunk : 2 * chunk], axis=0)
    scale = lax.rsqrt(total / (width * groups) + eps_norm)
    rows_out = got[:, :chunk, :].astype(F32) * scale[None, :, None]
    return rows_out.transpose(1, 0, 2).reshape(chunk, width * groups).astype(jnp.bfloat16)


def solution(mesh):
    fine = split_ctx(mesh)
    ctx = ("cy", "cx", "cc")
    spec = P(ctx, "head")
    in_specs = (spec, spec, spec, spec, spec, P())
    out_specs = P((*ctx, "head"), None)
    return jax.shard_map(body, mesh=fine, in_specs=in_specs, out_specs=out_specs, check_vma=False)
```

```python
import jax
import jax.numpy as jnp
from jax import lax
from jax.sharding import Mesh, PartitionSpec as P

eps_norm = 1e-05
HI = lax.Precision.HIGHEST
F32 = jnp.float32


def split_ctx(mesh):
    devices = mesh.devices
    ctx_devices = list(devices[:, 0])
    rows = len({d.coords[1] for d in ctx_devices})
    cols = len({d.coords[0] for d in ctx_devices})
    cores = len(ctx_devices) // (rows * cols)
    shape = (rows, cols, cores, devices.shape[1])
    return Mesh(devices.reshape(shape), ("cy", "cx", "cc", "head"))


def pack(log, state):
    row = jnp.broadcast_to(log[:, None, None], (state.shape[0], 1, state.shape[2]))
    return jnp.concatenate([state, row], axis=1)


def unpack(packed):
    return packed[:, -1, 0], packed[:, :-1]


def shifted(x, axis, n):
    out = [x]
    for s in range(1, n):
        out.append(lax.ppermute(x, axis, [(j, (j + s) % n) for j in range(n)]))
    return out


def scan_pieces(logs, states, i, n):
    log_before = jnp.zeros_like(logs[0])
    before = jnp.zeros_like(states[0])
    log_after = jnp.zeros_like(logs[0])
    after = jnp.zeros_like(states[0])
    for s in range(1, n):
        early = s <= i
        weight_b = jnp.where(early, jnp.exp(log_before), 0.0)
        weight_a = jnp.where(early, 0.0, jnp.exp(log_after))
        before = before + weight_b[:, None, None] * states[s]
        after = after + weight_a[:, None, None] * states[s]
        log_before = log_before + jnp.where(early, logs[s], 0.0)
        log_after = log_after + jnp.where(early, 0.0, logs[s])
    return log_before, before, log_after, after


def exclusive_scan(log, state, axis, n):
    def shift(packed, d):
        return lax.ppermute(packed, axis, [(j, j + d) for j in range(n - d)])

    cur_log, cur = unpack(shift(pack(log, state), 1))
    d = 1
    while d < n:
        got_log, got = unpack(shift(pack(cur_log, cur), d))
        cur = jnp.exp(cur_log)[:, None, None] * got + cur
        cur_log = cur_log + got_log
        d *= 2
    return cur_log, cur


def carried_state(L, S):
    rows, cols, cores = lax.axis_size("cy"), lax.axis_size("cx"), lax.axis_size("cc")
    y, x, c = lax.axis_index("cy"), lax.axis_index("cx"), lax.axis_index("cc")
    heads, size = S.shape[0], S.shape[1]
    group = heads // cores

    pair = unpack(lax.ppermute(pack(L, S), "cc", [(0, 1), (1, 0)]))
    L0 = jnp.where(c == 0, L, pair[0])
    S0 = jnp.where(c == 0, S, pair[1])
    L1 = jnp.where(c == 0, pair[0], L)
    S1 = jnp.where(c == 0, pair[1], S)
    chip_log = L0 + L1
    chip_state = jnp.exp(L1)[:, None, None] * S0 + S1
    g_log = lax.dynamic_slice_in_dim(chip_log, c * group, group, 0)
    g_state = lax.dynamic_slice_in_dim(chip_state, c * group, group, 0)

    row_pieces = [unpack(p) for p in shifted(pack(g_log, g_state), "cx", cols)]
    e_log, e_state, f_log, f_state = scan_pieces(
        [p[0] for p in row_pieces], [p[1] for p in row_pieces], x, cols
    )
    row_log = e_log + g_log + f_log
    row_state = jnp.exp(f_log)[:, None, None] * (jnp.exp(g_log)[:, None, None] * e_state + g_state) + f_state

    part = size // cols
    q_state = lax.dynamic_slice_in_dim(row_state, x * part, part, 1)
    y_log, y_state = exclusive_scan(row_log, q_state, "cy", rows)

    parts = shifted(y_state, "cx", cols)
    ordered = [lax.select_n((x - q) % cols, *parts) for q in range(cols)]
    y_full = jnp.concatenate(ordered, axis=1)

    chip_before = jnp.exp(e_log)[:, None, None] * y_full + e_state

    other = lax.ppermute(chip_before, "cc", [(0, 1), (1, 0)])
    full0 = jnp.concatenate([chip_before, other], axis=0)
    full1 = jnp.concatenate([other, chip_before], axis=0)
    chip_full = jnp.where(c == 0, full0, full1)
    return jnp.where(c == 0, chip_full, jnp.exp(L0)[:, None, None] * chip_full + S0)


def inner_head(qh, kh, vh, ch):
    count = qh.shape[0]
    target_index = jnp.arange(count)
    causal = target_index[:, None] >= target_index[None, :]
    scores = jnp.dot(qh, kh.T, preferred_element_type=F32)
    spread = jnp.where(causal, ch[:, None] - ch[None, :], 0.0)
    weights = (scores * jnp.where(causal, jnp.exp(spread), 0.0)).astype(jnp.bfloat16)
    return jnp.dot(weights, vh, preferred_element_type=F32)


def body(queries, keys, values, log_decay, gate, norm_gain):
    count, width = queries.shape
    heads = log_decay.shape[1]
    size = width // heads
    cum = jnp.cumsum(log_decay, axis=0)
    last = cum[-1]

    k3 = keys.reshape(count, heads, size)
    v3 = values.reshape(count, heads, size)
    q3 = queries.reshape(count, heads, size)
    keyed = k3.astype(F32) * jnp.exp(last[None, :] - cum)[:, :, None]
    state = jnp.einsum("thd,the->hde", keyed, v3.astype(F32), precision=HI)

    carried = carried_state(last, state)

    inner = jnp.stack(
        [inner_head(q3[:, h], k3[:, h], v3[:, h], cum[:, h]) for h in range(heads)], axis=1
    )
    across = jnp.einsum("thd,hde->the", q3.astype(F32), carried, precision=HI)
    attended = (inner + jnp.exp(cum)[:, :, None] * across).reshape(count, width).astype(jnp.bfloat16)

    groups = lax.axis_size("head")
    shade = attended.astype(F32)
    sums = jnp.sum(shade * shade, axis=1)
    gain = lax.dynamic_slice_in_dim(norm_gain, lax.axis_index("head") * width, width, 0)
    shaped = (shade * gain * jax.nn.sigmoid(gate.astype(F32))).astype(jnp.bfloat16)
    chunk = count // groups
    high = sums.astype(jnp.bfloat16)
    low = (sums - high.astype(F32)).astype(jnp.bfloat16)
    extra = jnp.zeros((groups, 1, width), jnp.bfloat16)
    extra = extra.at[:, 0, :chunk].set(high.reshape(groups, chunk))
    extra = extra.at[:, 0, chunk : 2 * chunk].set(low.reshape(groups, chunk))
    payload = jnp.concatenate([shaped.reshape(groups, chunk, width), extra], axis=1)
    got = lax.all_to_all(payload, "head", split_axis=0, concat_axis=0, tiled=True)
    parts = got[:, -1, :].astype(F32)
    total = jnp.sum(parts[:, :chunk] + parts[:, chunk : 2 * chunk], axis=0)
    scale = lax.rsqrt(total / (width * groups) + eps_norm)
    rows_out = got[:, :chunk, :].astype(F32) * scale[None, :, None]
    return rows_out.transpose(1, 0, 2).reshape(chunk, width * groups).astype(jnp.bfloat16)


def solution(mesh):
    fine = split_ctx(mesh)
    ctx = ("cy", "cx", "cc")
    spec = P(ctx, "head")
    in_specs = (spec, spec, spec, spec, spec, P())
    out_specs = P((*ctx, "head"), None)
    return jax.shard_map(body, mesh=fine, in_specs=in_specs, out_specs=out_specs, check_vma=False)
```

```python
import jax
import jax.numpy as jnp
from jax import lax
from jax.sharding import Mesh, PartitionSpec as P

eps_norm = 1e-05
HI = lax.Precision.HIGHEST
F32 = jnp.float32


def split_ctx(mesh):
    devices = mesh.devices
    ctx_devices = list(devices[:, 0])
    rows = len({d.coords[1] for d in ctx_devices})
    cols = len({d.coords[0] for d in ctx_devices})
    cores = len(ctx_devices) // (rows * cols)
    shape = (rows, cols, cores, devices.shape[1])
    return Mesh(devices.reshape(shape), ("cy", "cx", "cc", "head"))


def pack(log, state):
    row = jnp.broadcast_to(log[:, None, None], (state.shape[0], 1, state.shape[2]))
    return jnp.concatenate([state, row], axis=1)


def unpack(packed):
    return packed[:, -1, 0], packed[:, :-1]


def shifted(x, axis, n):
    out = [x]
    for s in range(1, n):
        out.append(lax.ppermute(x, axis, [(j, (j + s) % n) for j in range(n)]))
    return out


def scan_pieces(logs, states, i, n):
    log_before = jnp.zeros_like(logs[0])
    before = jnp.zeros_like(states[0])
    log_after = jnp.zeros_like(logs[0])
    after = jnp.zeros_like(states[0])
    for s in range(1, n):
        early = s <= i
        weight_b = jnp.where(early, jnp.exp(log_before), 0.0)
        weight_a = jnp.where(early, 0.0, jnp.exp(log_after))
        before = before + weight_b[:, None, None] * states[s]
        after = after + weight_a[:, None, None] * states[s]
        log_before = log_before + jnp.where(early, logs[s], 0.0)
        log_after = log_after + jnp.where(early, 0.0, logs[s])
    return log_before, before, log_after, after


def exclusive_scan(log, state, axis, n):
    def shift(packed, d):
        return lax.ppermute(packed, axis, [(j, j + d) for j in range(n - d)])

    cur_log, cur = unpack(shift(pack(log, state), 1))
    d = 1
    while d < n:
        got_log, got = unpack(shift(pack(cur_log, cur), d))
        cur = jnp.exp(cur_log)[:, None, None] * got + cur
        cur_log = cur_log + got_log
        d *= 2
    return cur_log, cur


def carried_state(L, S):
    rows, cols, cores = lax.axis_size("cy"), lax.axis_size("cx"), lax.axis_size("cc")
    y, x, c = lax.axis_index("cy"), lax.axis_index("cx"), lax.axis_index("cc")
    heads, size = S.shape[0], S.shape[1]
    group = heads // cores

    pair = unpack(lax.ppermute(pack(L, S), "cc", [(0, 1), (1, 0)]))
    L0 = jnp.where(c == 0, L, pair[0])
    S0 = jnp.where(c == 0, S, pair[1])
    L1 = jnp.where(c == 0, pair[0], L)
    S1 = jnp.where(c == 0, pair[1], S)
    chip_log = L0 + L1
    chip_state = jnp.exp(L1)[:, None, None] * S0 + S1
    g_log = lax.dynamic_slice_in_dim(chip_log, c * group, group, 0)
    g_state = lax.dynamic_slice_in_dim(chip_state, c * group, group, 0)

    row_pieces = [unpack(p) for p in shifted(pack(g_log, g_state), "cx", cols)]
    e_log, e_state, f_log, f_state = scan_pieces(
        [p[0] for p in row_pieces], [p[1] for p in row_pieces], x, cols
    )
    row_log = e_log + g_log + f_log
    row_state = jnp.exp(f_log)[:, None, None] * (jnp.exp(g_log)[:, None, None] * e_state + g_state) + f_state

    part = size // cols
    q_state = lax.dynamic_slice_in_dim(row_state, x * part, part, 1)
    y_log, y_state = exclusive_scan(row_log, q_state, "cy", rows)

    parts = shifted(y_state, "cx", cols)
    ordered = [lax.select_n((x - q) % cols, *parts) for q in range(cols)]
    y_full = jnp.concatenate(ordered, axis=1)

    chip_before = jnp.exp(e_log)[:, None, None] * y_full + e_state

    other = lax.ppermute(chip_before, "cc", [(0, 1), (1, 0)])
    full0 = jnp.concatenate([chip_before, other], axis=0)
    full1 = jnp.concatenate([other, chip_before], axis=0)
    chip_full = jnp.where(c == 0, full0, full1)
    return jnp.where(c == 0, chip_full, jnp.exp(L0)[:, None, None] * chip_full + S0)


def inner_head(qh, kh, vh, ch):
    count = qh.shape[0]
    target_index = jnp.arange(count)
    causal = target_index[:, None] >= target_index[None, :]
    scores = jnp.dot(qh, kh.T, preferred_element_type=F32)
    spread = jnp.where(causal, ch[:, None] - ch[None, :], 0.0)
    weights = (scores * jnp.where(causal, jnp.exp(spread), 0.0)).astype(jnp.bfloat16)
    return jnp.dot(weights, vh, preferred_element_type=F32)


def body(queries, keys, values, log_decay, gate, norm_gain):
    count, width = queries.shape
    heads = log_decay.shape[1]
    size = width // heads
    cum = jnp.cumsum(log_decay, axis=0)
    last = cum[-1]

    def cols(array, h):
        return array[:, h * size : (h + 1) * size]

    state = jnp.stack(
        [
            jnp.dot(
                (cols(keys, h).astype(F32) * jnp.exp(last[h] - cum[:, h])[:, None]).T,
                cols(values, h).astype(F32),
                precision=HI,
            )
            for h in range(heads)
        ]
    )

    carried = carried_state(last, state)

    joined = []
    for h in range(heads):
        qh = cols(queries, h)
        inner = inner_head(qh, cols(keys, h), cols(values, h), cum[:, h])
        across = jnp.dot(qh.astype(F32), carried[h], precision=HI)
        joined.append(inner + jnp.exp(cum[:, h])[:, None] * across)
    attended = jnp.concatenate(joined, axis=1).astype(jnp.bfloat16)

    groups = lax.axis_size("head")
    shade = attended.astype(F32)
    sums = jnp.sum(shade * shade, axis=1)
    gain = lax.dynamic_slice_in_dim(norm_gain, lax.axis_index("head") * width, width, 0)
    shaped = (shade * gain * jax.nn.sigmoid(gate.astype(F32))).astype(jnp.bfloat16)
    chunk = count // groups
    high = sums.astype(jnp.bfloat16)
    low = (sums - high.astype(F32)).astype(jnp.bfloat16)
    extra = jnp.concatenate(
        [
            high.reshape(groups, 1, chunk),
            low.reshape(groups, 1, chunk),
            jnp.zeros((groups, 1, width - 2 * chunk), jnp.bfloat16),
        ],
        axis=2,
    )
    payload = jnp.concatenate([shaped.reshape(groups, chunk, width), extra], axis=1)
    got = lax.all_to_all(payload, "head", split_axis=0, concat_axis=0, tiled=True)
    parts = got[:, -1, :].astype(F32)
    total = jnp.sum(parts[:, :chunk] + parts[:, chunk : 2 * chunk], axis=0)
    scale = lax.rsqrt(total / (width * groups) + eps_norm)
    rows_out = got[:, :chunk, :].astype(F32) * scale[None, :, None]
    return rows_out.transpose(1, 0, 2).reshape(chunk, width * groups).astype(jnp.bfloat16)


def solution(mesh):
    fine = split_ctx(mesh)
    ctx = ("cy", "cx", "cc")
    spec = P(ctx, "head")
    in_specs = (spec, spec, spec, spec, spec, P())
    out_specs = P((*ctx, "head"), None)
    return jax.shard_map(body, mesh=fine, in_specs=in_specs, out_specs=out_specs, check_vma=False)
```

```python
import jax
import jax.numpy as jnp
from jax import lax
from jax.sharding import Mesh, PartitionSpec as P

eps_norm = 1e-05
HI = lax.Precision.HIGHEST
F32 = jnp.float32


def split_ctx(mesh):
    devices = mesh.devices
    ctx_devices = list(devices[:, 0])
    rows = len({d.coords[1] for d in ctx_devices})
    cols = len({d.coords[0] for d in ctx_devices})
    cores = len(ctx_devices) // (rows * cols)
    shape = (rows, cols, cores, devices.shape[1])
    return Mesh(devices.reshape(shape), ("cy", "cx", "cc", "head"))


def pack(log, state):
    row = jnp.broadcast_to(log[:, None, None], (state.shape[0], 1, state.shape[2]))
    return jnp.concatenate([state, row], axis=1)


def unpack(packed):
    return packed[:, -1, 0], packed[:, :-1]


def shifted(x, axis, n):
    out = [x]
    for s in range(1, n):
        out.append(lax.ppermute(x, axis, [(j, (j + s) % n) for j in range(n)]))
    return out


def scan_pieces(logs, states, i, n):
    log_before = jnp.zeros_like(logs[0])
    before = jnp.zeros_like(states[0])
    log_after = jnp.zeros_like(logs[0])
    after = jnp.zeros_like(states[0])
    for s in range(1, n):
        early = s <= i
        weight_b = jnp.where(early, jnp.exp(log_before), 0.0)
        weight_a = jnp.where(early, 0.0, jnp.exp(log_after))
        before = before + weight_b[:, None, None] * states[s]
        after = after + weight_a[:, None, None] * states[s]
        log_before = log_before + jnp.where(early, logs[s], 0.0)
        log_after = log_after + jnp.where(early, 0.0, logs[s])
    return log_before, before, log_after, after


def exclusive_scan(log, state, axis, n):
    def shift(packed, d):
        return lax.ppermute(packed, axis, [(j, j + d) for j in range(n - d)])

    cur_log, cur = unpack(shift(pack(log, state), 1))
    d = 1
    while d < n:
        got_log, got = unpack(shift(pack(cur_log, cur), d))
        cur = jnp.exp(cur_log)[:, None, None] * got + cur
        cur_log = cur_log + got_log
        d *= 2
    return cur_log, cur


def carried_state(L, S):
    rows, cols, cores = lax.axis_size("cy"), lax.axis_size("cx"), lax.axis_size("cc")
    y, x, c = lax.axis_index("cy"), lax.axis_index("cx"), lax.axis_index("cc")
    heads, size = S.shape[0], S.shape[1]
    group = heads // cores

    pair = unpack(lax.ppermute(pack(L, S), "cc", [(0, 1), (1, 0)]))
    L0 = jnp.where(c == 0, L, pair[0])
    S0 = jnp.where(c == 0, S, pair[1])
    L1 = jnp.where(c == 0, pair[0], L)
    S1 = jnp.where(c == 0, pair[1], S)
    chip_log = L0 + L1
    chip_state = jnp.exp(L1)[:, None, None] * S0 + S1
    g_log = lax.dynamic_slice_in_dim(chip_log, c * group, group, 0)
    g_state = lax.dynamic_slice_in_dim(chip_state, c * group, group, 0)

    row_pieces = [unpack(p) for p in shifted(pack(g_log, g_state), "cx", cols)]
    e_log, e_state, f_log, f_state = scan_pieces(
        [p[0] for p in row_pieces], [p[1] for p in row_pieces], x, cols
    )
    row_log = e_log + g_log + f_log
    row_state = jnp.exp(f_log)[:, None, None] * (jnp.exp(g_log)[:, None, None] * e_state + g_state) + f_state

    part = size // cols
    q_state = lax.dynamic_slice_in_dim(row_state, x * part, part, 1)
    y_log, y_state = exclusive_scan(row_log, q_state, "cy", rows)

    parts = shifted(y_state, "cx", cols)
    ordered = [lax.select_n((x - q) % cols, *parts) for q in range(cols)]
    y_full = jnp.concatenate(ordered, axis=1)

    chip_before = jnp.exp(e_log)[:, None, None] * y_full + e_state

    other = lax.ppermute(chip_before, "cc", [(0, 1), (1, 0)])
    full0 = jnp.concatenate([chip_before, other], axis=0)
    full1 = jnp.concatenate([other, chip_before], axis=0)
    chip_full = jnp.where(c == 0, full0, full1)
    return jnp.where(c == 0, chip_full, jnp.exp(L0)[:, None, None] * chip_full + S0)


def inner_head(qh, kh, vh, ch):
    count = qh.shape[0]
    target_index = jnp.arange(count)
    causal = target_index[:, None] >= target_index[None, :]
    scores = jnp.dot(qh, kh.T, preferred_element_type=F32)
    spread = jnp.where(causal, ch[:, None] - ch[None, :], 0.0)
    weights = (scores * jnp.where(causal, jnp.exp(spread), 0.0)).astype(jnp.bfloat16)
    return jnp.dot(weights, vh, preferred_element_type=F32)


def body(queries, keys, values, log_decay, gate, norm_gain):
    count, width = queries.shape
    heads = log_decay.shape[1]
    size = width // heads
    cum = jnp.cumsum(log_decay, axis=0)
    last = cum[-1]

    def cols(array, h):
        return array[:, h * size : (h + 1) * size]

    k3 = keys.reshape(count, heads, size).astype(F32)
    keyed = k3 * jnp.exp(last[None, :] - cum)[:, :, None]
    state = jnp.einsum("thd,the->hde", keyed, values.reshape(count, heads, size).astype(F32), precision=HI)

    carried = carried_state(last, state)

    joined = []
    for h in range(heads):
        qh = cols(queries, h)
        inner = inner_head(qh, cols(keys, h), cols(values, h), cum[:, h])
        across = jnp.dot(qh.astype(F32), carried[h], precision=HI)
        joined.append(inner + jnp.exp(cum[:, h])[:, None] * across)
    attended = jnp.concatenate(joined, axis=1).astype(jnp.bfloat16)

    groups = lax.axis_size("head")
    shade = attended.astype(F32)
    sums = jnp.sum(shade * shade, axis=1)
    gain = lax.dynamic_slice_in_dim(norm_gain, lax.axis_index("head") * width, width, 0)
    shaped = (shade * gain * jax.nn.sigmoid(gate.astype(F32))).astype(jnp.bfloat16)
    chunk = count // groups
    high = sums.astype(jnp.bfloat16)
    low = (sums - high.astype(F32)).astype(jnp.bfloat16)
    extra = jnp.concatenate(
        [
            high.reshape(groups, 1, chunk),
            low.reshape(groups, 1, chunk),
            jnp.zeros((groups, 1, width - 2 * chunk), jnp.bfloat16),
        ],
        axis=2,
    )
    payload = jnp.concatenate([shaped.reshape(groups, chunk, width), extra], axis=1)
    got = lax.all_to_all(payload, "head", split_axis=0, concat_axis=0, tiled=True)
    parts = got[:, -1, :].astype(F32)
    total = jnp.sum(parts[:, :chunk] + parts[:, chunk : 2 * chunk], axis=0)
    scale = lax.rsqrt(total / (width * groups) + eps_norm)
    rows_out = got[:, :chunk, :].astype(F32) * scale[None, :, None]
    return rows_out.transpose(1, 0, 2).reshape(chunk, width * groups).astype(jnp.bfloat16)


def solution(mesh):
    fine = split_ctx(mesh)
    ctx = ("cy", "cx", "cc")
    spec = P(ctx, "head")
    in_specs = (spec, spec, spec, spec, spec, P())
    out_specs = P((*ctx, "head"), None)
    return jax.shard_map(body, mesh=fine, in_specs=in_specs, out_specs=out_specs, check_vma=False)
```

```python
import jax
import jax.numpy as jnp
from jax import lax
from jax.sharding import Mesh, PartitionSpec as P

eps_norm = 1e-05
HI = lax.Precision.HIGHEST
F32 = jnp.float32


def split_ctx(mesh):
    devices = mesh.devices
    ctx_devices = list(devices[:, 0])
    rows = len({d.coords[1] for d in ctx_devices})
    cols = len({d.coords[0] for d in ctx_devices})
    cores = len(ctx_devices) // (rows * cols)
    shape = (rows, cols, cores, devices.shape[1])
    return Mesh(devices.reshape(shape), ("cy", "cx", "cc", "head"))


def pack(log, state):
    row = jnp.broadcast_to(log[:, None, None], (state.shape[0], 1, state.shape[2]))
    return jnp.concatenate([state, row], axis=1)


def unpack(packed):
    return packed[:, -1, 0], packed[:, :-1]


def shifted(x, axis, n):
    out = [x]
    for s in range(1, n):
        out.append(lax.ppermute(x, axis, [(j, (j + s) % n) for j in range(n)]))
    return out


def scan_pieces(logs, states, i, n):
    log_before = jnp.zeros_like(logs[0])
    before = jnp.zeros_like(states[0])
    log_after = jnp.zeros_like(logs[0])
    after = jnp.zeros_like(states[0])
    for s in range(1, n):
        early = s <= i
        weight_b = jnp.where(early, jnp.exp(log_before), 0.0)
        weight_a = jnp.where(early, 0.0, jnp.exp(log_after))
        before = before + weight_b[:, None, None] * states[s]
        after = after + weight_a[:, None, None] * states[s]
        log_before = log_before + jnp.where(early, logs[s], 0.0)
        log_after = log_after + jnp.where(early, 0.0, logs[s])
    return log_before, before, log_after, after


def exclusive_scan(log, state, axis, n):
    def shift(packed, d):
        return lax.ppermute(packed, axis, [(j, j + d) for j in range(n - d)])

    packed = pack(log, state)
    one_log, one = unpack(shift(packed, 1))
    two_log, two = unpack(shift(packed, 2))
    cur = jnp.exp(one_log)[:, None, None] * two + one
    cur_log = one_log + two_log
    d = 2
    while d < n:
        got_log, got = unpack(shift(pack(cur_log, cur), d))
        cur = jnp.exp(cur_log)[:, None, None] * got + cur
        cur_log = cur_log + got_log
        d *= 2
    return cur_log, cur


def carried_state(L, S):
    rows, cols, cores = lax.axis_size("cy"), lax.axis_size("cx"), lax.axis_size("cc")
    y, x, c = lax.axis_index("cy"), lax.axis_index("cx"), lax.axis_index("cc")
    heads, size = S.shape[0], S.shape[1]
    group = heads // cores

    pair = unpack(lax.ppermute(pack(L, S), "cc", [(0, 1), (1, 0)]))
    L0 = jnp.where(c == 0, L, pair[0])
    S0 = jnp.where(c == 0, S, pair[1])
    L1 = jnp.where(c == 0, pair[0], L)
    S1 = jnp.where(c == 0, pair[1], S)
    chip_log = L0 + L1
    chip_state = jnp.exp(L1)[:, None, None] * S0 + S1
    g_log = lax.dynamic_slice_in_dim(chip_log, c * group, group, 0)
    g_state = lax.dynamic_slice_in_dim(chip_state, c * group, group, 0)

    row_pieces = [unpack(p) for p in shifted(pack(g_log, g_state), "cx", cols)]
    e_log, e_state, f_log, f_state = scan_pieces(
        [p[0] for p in row_pieces], [p[1] for p in row_pieces], x, cols
    )
    row_log = e_log + g_log + f_log
    row_state = jnp.exp(f_log)[:, None, None] * (jnp.exp(g_log)[:, None, None] * e_state + g_state) + f_state

    part = size // cols
    q_state = lax.dynamic_slice_in_dim(row_state, x * part, part, 1)
    y_log, y_state = exclusive_scan(row_log, q_state, "cy", rows)

    parts = shifted(y_state, "cx", cols)
    ordered = [lax.select_n((x - q) % cols, *parts) for q in range(cols)]
    y_full = jnp.concatenate(ordered, axis=1)

    chip_before = jnp.exp(e_log)[:, None, None] * y_full + e_state

    other = lax.ppermute(chip_before, "cc", [(0, 1), (1, 0)])
    full0 = jnp.concatenate([chip_before, other], axis=0)
    full1 = jnp.concatenate([other, chip_before], axis=0)
    chip_full = jnp.where(c == 0, full0, full1)
    return jnp.where(c == 0, chip_full, jnp.exp(L0)[:, None, None] * chip_full + S0)


def inner_head(qh, kh, vh, ch):
    count = qh.shape[0]
    target_index = jnp.arange(count)
    causal = target_index[:, None] >= target_index[None, :]
    scores = jnp.dot(qh, kh.T, preferred_element_type=F32)
    spread = jnp.where(causal, ch[:, None] - ch[None, :], 0.0)
    weights = (scores * jnp.where(causal, jnp.exp(spread), 0.0)).astype(jnp.bfloat16)
    return jnp.dot(weights, vh, preferred_element_type=F32)


def body(queries, keys, values, log_decay, gate, norm_gain):
    count, width = queries.shape
    heads = log_decay.shape[1]
    size = width // heads
    cum = jnp.cumsum(log_decay, axis=0)
    last = cum[-1]

    def cols(array, h):
        return array[:, h * size : (h + 1) * size]

    state = jnp.stack(
        [
            jnp.dot(
                (cols(keys, h).astype(F32) * jnp.exp(last[h] - cum[:, h])[:, None]).T,
                cols(values, h).astype(F32),
                precision=HI,
            )
            for h in range(heads)
        ]
    )

    carried = carried_state(last, state)

    joined = []
    for h in range(heads):
        qh = cols(queries, h)
        inner = inner_head(qh, cols(keys, h), cols(values, h), cum[:, h])
        across = jnp.dot(qh.astype(F32), carried[h], precision=HI)
        joined.append(inner + jnp.exp(cum[:, h])[:, None] * across)
    attended = jnp.concatenate(joined, axis=1).astype(jnp.bfloat16)

    groups = lax.axis_size("head")
    shade = attended.astype(F32)
    sums = jnp.sum(shade * shade, axis=1)
    gain = lax.dynamic_slice_in_dim(norm_gain, lax.axis_index("head") * width, width, 0)
    shaped = (shade * gain * jax.nn.sigmoid(gate.astype(F32))).astype(jnp.bfloat16)
    chunk = count // groups
    high = sums.astype(jnp.bfloat16)
    low = (sums - high.astype(F32)).astype(jnp.bfloat16)
    extra = jnp.concatenate(
        [
            high.reshape(groups, 1, chunk),
            low.reshape(groups, 1, chunk),
            jnp.zeros((groups, 1, width - 2 * chunk), jnp.bfloat16),
        ],
        axis=2,
    )
    payload = jnp.concatenate([shaped.reshape(groups, chunk, width), extra], axis=1)
    got = lax.all_to_all(payload, "head", split_axis=0, concat_axis=0, tiled=True)
    parts = got[:, -1, :].astype(F32)
    total = jnp.sum(parts[:, :chunk] + parts[:, chunk : 2 * chunk], axis=0)
    scale = lax.rsqrt(total / (width * groups) + eps_norm)
    rows_out = got[:, :chunk, :].astype(F32) * scale[None, :, None]
    return rows_out.transpose(1, 0, 2).reshape(chunk, width * groups).astype(jnp.bfloat16)


def solution(mesh):
    fine = split_ctx(mesh)
    ctx = ("cy", "cx", "cc")
    spec = P(ctx, "head")
    in_specs = (spec, spec, spec, spec, spec, P())
    out_specs = P((*ctx, "head"), None)
    return jax.shard_map(body, mesh=fine, in_specs=in_specs, out_specs=out_specs, check_vma=False)
```

```python
import jax
import jax.numpy as jnp
from jax import lax
from jax.sharding import Mesh, PartitionSpec as P

eps_norm = 1e-05
HI = lax.Precision.HIGHEST
F32 = jnp.float32


def split_ctx(mesh):
    devices = mesh.devices
    ctx_devices = list(devices[:, 0])
    rows = len({d.coords[1] for d in ctx_devices})
    cols = len({d.coords[0] for d in ctx_devices})
    cores = len(ctx_devices) // (rows * cols)
    shape = (rows, cols, cores, devices.shape[1])
    return Mesh(devices.reshape(shape), ("cy", "cx", "cc", "head"))


def pack(log, state):
    row = jnp.broadcast_to(log[:, None, None], (state.shape[0], 1, state.shape[2]))
    return jnp.concatenate([state, row], axis=1)


def unpack(packed):
    return packed[:, -1, 0], packed[:, :-1]


def shifted(x, axis, n):
    out = [x]
    for s in range(1, n):
        out.append(lax.ppermute(x, axis, [(j, (j + s) % n) for j in range(n)]))
    return out


def scan_pieces(logs, states, i, n):
    log_before = jnp.zeros_like(logs[0])
    before = jnp.zeros_like(states[0])
    log_after = jnp.zeros_like(logs[0])
    after = jnp.zeros_like(states[0])
    for s in range(1, n):
        early = s <= i
        weight_b = jnp.where(early, jnp.exp(log_before), 0.0)
        weight_a = jnp.where(early, 0.0, jnp.exp(log_after))
        before = before + weight_b[:, None, None] * states[s]
        after = after + weight_a[:, None, None] * states[s]
        log_before = log_before + jnp.where(early, logs[s], 0.0)
        log_after = log_after + jnp.where(early, 0.0, logs[s])
    return log_before, before, log_after, after


def exclusive_scan(log, state, axis, n):
    def shift(packed, d):
        return lax.ppermute(packed, axis, [(j, j + d) for j in range(n - d)])

    packed = pack(log, state)
    one_log, one = unpack(shift(packed, 1))
    two_log, two = unpack(shift(packed, 2))
    cur = jnp.exp(one_log)[:, None, None] * two + one
    cur_log = one_log + two_log
    d = 2
    while d < n:
        got_log, got = unpack(shift(pack(cur_log, cur), d))
        cur = jnp.exp(cur_log)[:, None, None] * got + cur
        cur_log = cur_log + got_log
        d *= 2
    return cur_log, cur


def carried_state(L, S):
    rows, cols, cores = lax.axis_size("cy"), lax.axis_size("cx"), lax.axis_size("cc")
    y, x, c = lax.axis_index("cy"), lax.axis_index("cx"), lax.axis_index("cc")
    heads, size = S.shape[0], S.shape[1]

    pair = unpack(lax.ppermute(pack(L, S), "cc", [(0, 1), (1, 0)]))
    L0 = jnp.where(c == 0, L, pair[0])
    S0 = jnp.where(c == 0, S, pair[1])
    L1 = jnp.where(c == 0, pair[0], L)
    S1 = jnp.where(c == 0, pair[1], S)
    chip_log = L0 + L1
    chip_state = jnp.exp(L1)[:, None, None] * S0 + S1
    row_pieces = [unpack(p) for p in shifted(pack(chip_log, chip_state), "cx", cols)]
    e_log, e_state, f_log, f_state = scan_pieces(
        [p[0] for p in row_pieces], [p[1] for p in row_pieces], x, cols
    )
    row_log = e_log + chip_log + f_log
    row_state = jnp.exp(f_log)[:, None, None] * (jnp.exp(chip_log)[:, None, None] * e_state + chip_state) + f_state

    part = size // cols
    q_state = lax.dynamic_slice_in_dim(row_state, x * part, part, 1)
    y_log, y_state = exclusive_scan(row_log, q_state, "cy", rows)

    parts = shifted(y_state, "cx", cols)
    ordered = [lax.select_n((x - q) % cols, *parts) for q in range(cols)]
    y_full = jnp.concatenate(ordered, axis=1)

    chip_before = jnp.exp(e_log)[:, None, None] * y_full + e_state
    return jnp.where(c == 0, chip_before, jnp.exp(L0)[:, None, None] * chip_before + S0)


def inner_head(qh, kh, vh, ch):
    count = qh.shape[0]
    target_index = jnp.arange(count)
    causal = target_index[:, None] >= target_index[None, :]
    scores = jnp.dot(qh, kh.T, preferred_element_type=F32)
    spread = jnp.where(causal, ch[:, None] - ch[None, :], 0.0)
    weights = (scores * jnp.where(causal, jnp.exp(spread), 0.0)).astype(jnp.bfloat16)
    return jnp.dot(weights, vh, preferred_element_type=F32)


def body(queries, keys, values, log_decay, gate, norm_gain):
    count, width = queries.shape
    heads = log_decay.shape[1]
    size = width // heads
    cum = jnp.cumsum(log_decay, axis=0)
    last = cum[-1]

    def cols(array, h):
        return array[:, h * size : (h + 1) * size]

    state = jnp.stack(
        [
            jnp.dot(
                (cols(keys, h).astype(F32) * jnp.exp(last[h] - cum[:, h])[:, None]).T,
                cols(values, h).astype(F32),
                precision=HI,
            )
            for h in range(heads)
        ]
    )

    carried = carried_state(last, state)

    joined = []
    for h in range(heads):
        qh = cols(queries, h)
        inner = inner_head(qh, cols(keys, h), cols(values, h), cum[:, h])
        across = jnp.dot(qh.astype(F32), carried[h], precision=HI)
        joined.append(inner + jnp.exp(cum[:, h])[:, None] * across)
    attended = jnp.concatenate(joined, axis=1).astype(jnp.bfloat16)

    groups = lax.axis_size("head")
    shade = attended.astype(F32)
    sums = jnp.sum(shade * shade, axis=1)
    gain = lax.dynamic_slice_in_dim(norm_gain, lax.axis_index("head") * width, width, 0)
    shaped = (shade * gain * jax.nn.sigmoid(gate.astype(F32))).astype(jnp.bfloat16)
    chunk = count // groups
    high = sums.astype(jnp.bfloat16)
    low = (sums - high.astype(F32)).astype(jnp.bfloat16)
    extra = jnp.concatenate(
        [
            high.reshape(groups, 1, chunk),
            low.reshape(groups, 1, chunk),
            jnp.zeros((groups, 1, width - 2 * chunk), jnp.bfloat16),
        ],
        axis=2,
    )
    payload = jnp.concatenate([shaped.reshape(groups, chunk, width), extra], axis=1)
    got = lax.all_to_all(payload, "head", split_axis=0, concat_axis=0, tiled=True)
    parts = got[:, -1, :].astype(F32)
    total = jnp.sum(parts[:, :chunk] + parts[:, chunk : 2 * chunk], axis=0)
    scale = lax.rsqrt(total / (width * groups) + eps_norm)
    rows_out = got[:, :chunk, :].astype(F32) * scale[None, :, None]
    return rows_out.transpose(1, 0, 2).reshape(chunk, width * groups).astype(jnp.bfloat16)


def solution(mesh):
    fine = split_ctx(mesh)
    ctx = ("cy", "cx", "cc")
    spec = P(ctx, "head")
    in_specs = (spec, spec, spec, spec, spec, P())
    out_specs = P((*ctx, "head"), None)
    return jax.shard_map(body, mesh=fine, in_specs=in_specs, out_specs=out_specs, check_vma=False)
```

```python
import jax
import jax.numpy as jnp
from jax import lax
from jax.sharding import Mesh, PartitionSpec as P

eps_norm = 1e-05
HI = lax.Precision.HIGHEST
F32 = jnp.float32


def split_ctx(mesh):
    devices = mesh.devices
    ctx_devices = list(devices[:, 0])
    rows = len({d.coords[1] for d in ctx_devices})
    cols = len({d.coords[0] for d in ctx_devices})
    cores = len(ctx_devices) // (rows * cols)
    shape = (rows, cols, cores, devices.shape[1])
    return Mesh(devices.reshape(shape), ("cy", "cx", "cc", "head"))


def pack(log, state):
    row = jnp.broadcast_to(log[:, None, None], (state.shape[0], 1, state.shape[2]))
    return jnp.concatenate([state, row], axis=1)


def unpack(packed):
    return packed[:, -1, 0], packed[:, :-1]


def shifted(x, axis, n):
    out = [x]
    for s in range(1, n):
        out.append(lax.ppermute(x, axis, [(j, (j + s) % n) for j in range(n)]))
    return out


def scan_pieces(logs, states, i, n):
    log_before = jnp.zeros_like(logs[0])
    before = jnp.zeros_like(states[0])
    log_after = jnp.zeros_like(logs[0])
    after = jnp.zeros_like(states[0])
    for s in range(1, n):
        early = s <= i
        weight_b = jnp.where(early, jnp.exp(log_before), 0.0)
        weight_a = jnp.where(early, 0.0, jnp.exp(log_after))
        before = before + weight_b[:, None, None] * states[s]
        after = after + weight_a[:, None, None] * states[s]
        log_before = log_before + jnp.where(early, logs[s], 0.0)
        log_after = log_after + jnp.where(early, 0.0, logs[s])
    return log_before, before, log_after, after


def exclusive_scan(log, state, axis, n):
    def shift(packed, d):
        return lax.ppermute(packed, axis, [(j, j + d) for j in range(n - d)])

    packed = pack(log, state)
    first = min(4, n - 1)
    cur_log = jnp.zeros_like(log)
    cur = jnp.zeros_like(state)
    for d in range(1, first + 1):
        got_log, got = unpack(shift(packed, d))
        cur = cur + jnp.exp(cur_log)[:, None, None] * got
        cur_log = cur_log + got_log
    d = first
    while d < n:
        got_log, got = unpack(shift(pack(cur_log, cur), d))
        cur = jnp.exp(cur_log)[:, None, None] * got + cur
        cur_log = cur_log + got_log
        d *= 2
    return cur_log, cur


def carried_state(L, S):
    rows, cols, cores = lax.axis_size("cy"), lax.axis_size("cx"), lax.axis_size("cc")
    y, x, c = lax.axis_index("cy"), lax.axis_index("cx"), lax.axis_index("cc")
    heads, size = S.shape[0], S.shape[1]
    group = heads // cores

    pair = unpack(lax.ppermute(pack(L, S), "cc", [(0, 1), (1, 0)]))
    L0 = jnp.where(c == 0, L, pair[0])
    S0 = jnp.where(c == 0, S, pair[1])
    L1 = jnp.where(c == 0, pair[0], L)
    S1 = jnp.where(c == 0, pair[1], S)
    chip_log = L0 + L1
    chip_state = jnp.exp(L1)[:, None, None] * S0 + S1
    g_log = lax.dynamic_slice_in_dim(chip_log, c * group, group, 0)
    g_state = lax.dynamic_slice_in_dim(chip_state, c * group, group, 0)

    row_pieces = [unpack(p) for p in shifted(pack(g_log, g_state), "cx", cols)]
    e_log, e_state, f_log, f_state = scan_pieces(
        [p[0] for p in row_pieces], [p[1] for p in row_pieces], x, cols
    )
    row_log = e_log + g_log + f_log
    row_state = jnp.exp(f_log)[:, None, None] * (jnp.exp(g_log)[:, None, None] * e_state + g_state) + f_state

    part = size // cols
    q_state = lax.dynamic_slice_in_dim(row_state, x * part, part, 1)
    y_log, y_state = exclusive_scan(row_log, q_state, "cy", rows)

    parts = shifted(y_state, "cx", cols)
    ordered = [lax.select_n((x - q) % cols, *parts) for q in range(cols)]
    y_full = jnp.concatenate(ordered, axis=1)

    chip_before = jnp.exp(e_log)[:, None, None] * y_full + e_state

    other = lax.ppermute(chip_before, "cc", [(0, 1), (1, 0)])
    full0 = jnp.concatenate([chip_before, other], axis=0)
    full1 = jnp.concatenate([other, chip_before], axis=0)
    chip_full = jnp.where(c == 0, full0, full1)
    return jnp.where(c == 0, chip_full, jnp.exp(L0)[:, None, None] * chip_full + S0)


def inner_head(qh, kh, vh, ch):
    count = qh.shape[0]
    target_index = jnp.arange(count)
    causal = target_index[:, None] >= target_index[None, :]
    scores = jnp.dot(qh, kh.T, preferred_element_type=F32)
    spread = jnp.where(causal, ch[:, None] - ch[None, :], 0.0)
    weights = (scores * jnp.where(causal, jnp.exp(spread), 0.0)).astype(jnp.bfloat16)
    return jnp.dot(weights, vh, preferred_element_type=F32)


def body(queries, keys, values, log_decay, gate, norm_gain):
    count, width = queries.shape
    heads = log_decay.shape[1]
    size = width // heads
    cum = jnp.cumsum(log_decay, axis=0)
    last = cum[-1]

    def cols(array, h):
        return array[:, h * size : (h + 1) * size]

    state = jnp.stack(
        [
            jnp.dot(
                (cols(keys, h).astype(F32) * jnp.exp(last[h] - cum[:, h])[:, None]).T,
                cols(values, h).astype(F32),
                precision=HI,
            )
            for h in range(heads)
        ]
    )

    carried = carried_state(last, state)

    joined = []
    for h in range(heads):
        qh = cols(queries, h)
        inner = inner_head(qh, cols(keys, h), cols(values, h), cum[:, h])
        across = jnp.dot(qh.astype(F32), carried[h], precision=HI)
        joined.append(inner + jnp.exp(cum[:, h])[:, None] * across)
    attended = jnp.concatenate(joined, axis=1).astype(jnp.bfloat16)

    groups = lax.axis_size("head")
    shade = attended.astype(F32)
    sums = jnp.sum(shade * shade, axis=1)
    gain = lax.dynamic_slice_in_dim(norm_gain, lax.axis_index("head") * width, width, 0)
    shaped = (shade * gain * jax.nn.sigmoid(gate.astype(F32))).astype(jnp.bfloat16)
    chunk = count // groups
    high = sums.astype(jnp.bfloat16)
    low = (sums - high.astype(F32)).astype(jnp.bfloat16)
    extra = jnp.concatenate(
        [
            high.reshape(groups, 1, chunk),
            low.reshape(groups, 1, chunk),
            jnp.zeros((groups, 1, width - 2 * chunk), jnp.bfloat16),
        ],
        axis=2,
    )
    payload = jnp.concatenate([shaped.reshape(groups, chunk, width), extra], axis=1)
    got = lax.all_to_all(payload, "head", split_axis=0, concat_axis=0, tiled=True)
    parts = got[:, -1, :].astype(F32)
    total = jnp.sum(parts[:, :chunk] + parts[:, chunk : 2 * chunk], axis=0)
    scale = lax.rsqrt(total / (width * groups) + eps_norm)
    rows_out = got[:, :chunk, :].astype(F32) * scale[None, :, None]
    return rows_out.transpose(1, 0, 2).reshape(chunk, width * groups).astype(jnp.bfloat16)


def solution(mesh):
    fine = split_ctx(mesh)
    ctx = ("cy", "cx", "cc")
    spec = P(ctx, "head")
    in_specs = (spec, spec, spec, spec, spec, P())
    out_specs = P((*ctx, "head"), None)
    return jax.shard_map(body, mesh=fine, in_specs=in_specs, out_specs=out_specs, check_vma=False)
```

```python
import jax
import jax.numpy as jnp
from jax import lax
from jax.sharding import Mesh, PartitionSpec as P

eps_norm = 1e-05
HI = lax.Precision.HIGHEST
F32 = jnp.float32


def split_ctx(mesh):
    devices = mesh.devices
    ctx_devices = list(devices[:, 0])
    rows = len({d.coords[1] for d in ctx_devices})
    cols = len({d.coords[0] for d in ctx_devices})
    cores = len(ctx_devices) // (rows * cols)
    shape = (rows, cols, cores, devices.shape[1])
    return Mesh(devices.reshape(shape), ("cy", "cx", "cc", "head"))


def pack(log, state):
    row = jnp.broadcast_to(log[:, None, None], (state.shape[0], 1, state.shape[2]))
    return jnp.concatenate([state, row], axis=1)


def unpack(packed):
    return packed[:, -1, 0], packed[:, :-1]


def shifted(x, axis, n):
    out = [x]
    for s in range(1, n):
        out.append(lax.ppermute(x, axis, [(j, (j + s) % n) for j in range(n)]))
    return out


def scan_pieces(logs, states, i, n):
    log_before = jnp.zeros_like(logs[0])
    before = jnp.zeros_like(states[0])
    log_after = jnp.zeros_like(logs[0])
    after = jnp.zeros_like(states[0])
    for s in range(1, n):
        early = s <= i
        weight_b = jnp.where(early, jnp.exp(log_before), 0.0)
        weight_a = jnp.where(early, 0.0, jnp.exp(log_after))
        before = before + weight_b[:, None, None] * states[s]
        after = after + weight_a[:, None, None] * states[s]
        log_before = log_before + jnp.where(early, logs[s], 0.0)
        log_after = log_after + jnp.where(early, 0.0, logs[s])
    return log_before, before, log_after, after


def exclusive_scan(log, state, axis, n):
    def shift(packed, d):
        return lax.ppermute(packed, axis, [(j, j + d) for j in range(n - d)])

    packed = pack(log, state)
    first = min(4, n - 1)
    cur_log = jnp.zeros_like(log)
    cur = jnp.zeros_like(state)
    for d in range(1, first + 1):
        got_log, got = unpack(shift(packed, d))
        cur = cur + jnp.exp(cur_log)[:, None, None] * got
        cur_log = cur_log + got_log
    d = first
    while d < n:
        got_log, got = unpack(shift(pack(cur_log, cur), d))
        cur = jnp.exp(cur_log)[:, None, None] * got + cur
        cur_log = cur_log + got_log
        d *= 2
    return cur_log, cur


def carried_state(L, S):
    rows, cols, cores = lax.axis_size("cy"), lax.axis_size("cx"), lax.axis_size("cc")
    y, x, c = lax.axis_index("cy"), lax.axis_index("cx"), lax.axis_index("cc")
    heads, size = S.shape[0], S.shape[1]
    group = heads // cores

    pair = unpack(lax.ppermute(pack(L, S), "cc", [(0, 1), (1, 0)]))
    L0 = jnp.where(c == 0, L, pair[0])
    S0 = jnp.where(c == 0, S, pair[1])
    L1 = jnp.where(c == 0, pair[0], L)
    S1 = jnp.where(c == 0, pair[1], S)
    chip_log = L0 + L1
    chip_state = jnp.exp(L1)[:, None, None] * S0 + S1
    g_log = lax.dynamic_slice_in_dim(chip_log, c * group, group, 0)
    g_state = lax.dynamic_slice_in_dim(chip_state, c * group, group, 0)

    row_pieces = [unpack(p) for p in shifted(pack(g_log, g_state), "cx", cols)]
    e_log, e_state, f_log, f_state = scan_pieces(
        [p[0] for p in row_pieces], [p[1] for p in row_pieces], x, cols
    )
    row_log = e_log + g_log + f_log
    row_state = jnp.exp(f_log)[:, None, None] * (jnp.exp(g_log)[:, None, None] * e_state + g_state) + f_state

    part = size // cols
    q_state = lax.dynamic_slice_in_dim(row_state, x * part, part, 1)
    y_log, y_state = exclusive_scan(row_log, q_state, "cy", rows)

    parts = shifted(y_state, "cx", cols)
    ordered = [lax.select_n((x - q) % cols, *parts) for q in range(cols)]
    y_full = jnp.concatenate(ordered, axis=1)

    chip_before = jnp.exp(e_log)[:, None, None] * y_full + e_state

    other = lax.ppermute(chip_before, "cc", [(0, 1), (1, 0)])
    full0 = jnp.concatenate([chip_before, other], axis=0)
    full1 = jnp.concatenate([other, chip_before], axis=0)
    chip_full = jnp.where(c == 0, full0, full1)
    return jnp.where(c == 0, chip_full, jnp.exp(L0)[:, None, None] * chip_full + S0)


def inner_head(qh, kh, vh, ch):
    count = qh.shape[0]
    target_index = jnp.arange(count)
    causal = target_index[:, None] >= target_index[None, :]
    scores = jnp.dot(qh, kh.T, preferred_element_type=F32)
    spread = jnp.where(causal, ch[:, None] - ch[None, :], 0.0)
    weights = (scores * jnp.where(causal, jnp.exp(spread), 0.0)).astype(jnp.bfloat16)
    return jnp.dot(weights, vh, preferred_element_type=F32)


def body(queries, keys, values, log_decay, gate, norm_gain):
    count, width = queries.shape
    heads = log_decay.shape[1]
    size = width // heads
    cum = jnp.cumsum(log_decay, axis=0)
    last = cum[-1]

    def cols(array, h):
        return array[:, h * size : (h + 1) * size]

    keyed = keys.reshape(count, heads, size).astype(F32) * jnp.exp(last[None, :] - cum)[:, :, None]
    state = jnp.einsum("thd,the->hde", keyed, values.reshape(count, heads, size).astype(F32), precision=HI)

    carried = carried_state(last, state)

    joined = []
    for h in range(heads):
        qh = cols(queries, h)
        inner = inner_head(qh, cols(keys, h), cols(values, h), cum[:, h])
        across = jnp.dot(qh.astype(F32), carried[h], precision=HI)
        joined.append(inner + jnp.exp(cum[:, h])[:, None] * across)
    attended = jnp.concatenate(joined, axis=1).astype(jnp.bfloat16)

    groups = lax.axis_size("head")
    shade = attended.astype(F32)
    sums = jnp.sum(shade * shade, axis=1)
    gain = lax.dynamic_slice_in_dim(norm_gain, lax.axis_index("head") * width, width, 0)
    shaped = (shade * gain * jax.nn.sigmoid(gate.astype(F32))).astype(jnp.bfloat16)
    chunk = count // groups
    high = sums.astype(jnp.bfloat16)
    low = (sums - high.astype(F32)).astype(jnp.bfloat16)
    extra = jnp.concatenate(
        [
            high.reshape(groups, 1, chunk),
            low.reshape(groups, 1, chunk),
            jnp.zeros((groups, 1, width - 2 * chunk), jnp.bfloat16),
        ],
        axis=2,
    )
    payload = jnp.concatenate([shaped.reshape(groups, chunk, width), extra], axis=1)
    got = lax.all_to_all(payload, "head", split_axis=0, concat_axis=0, tiled=True)
    parts = got[:, -1, :].astype(F32)
    total = jnp.sum(parts[:, :chunk] + parts[:, chunk : 2 * chunk], axis=0)
    scale = lax.rsqrt(total / (width * groups) + eps_norm)
    rows_out = got[:, :chunk, :].astype(F32) * scale[None, :, None]
    return rows_out.transpose(1, 0, 2).reshape(chunk, width * groups).astype(jnp.bfloat16)


def solution(mesh):
    fine = split_ctx(mesh)
    ctx = ("cy", "cx", "cc")
    spec = P(ctx, "head")
    in_specs = (spec, spec, spec, spec, spec, P())
    out_specs = P((*ctx, "head"), None)
    return jax.shard_map(body, mesh=fine, in_specs=in_specs, out_specs=out_specs, check_vma=False)
```

```python
import jax
import jax.numpy as jnp
from jax import lax
from jax.sharding import Mesh, PartitionSpec as P

eps_norm = 1e-05
HI = lax.Precision.HIGHEST
F32 = jnp.float32


def split_ctx(mesh):
    devices = mesh.devices
    ctx_devices = list(devices[:, 0])
    rows = len({d.coords[1] for d in ctx_devices})
    cols = len({d.coords[0] for d in ctx_devices})
    cores = len(ctx_devices) // (rows * cols)
    shape = (rows, cols, cores, devices.shape[1])
    return Mesh(devices.reshape(shape), ("cy", "cx", "cc", "head"))


def pack(log, state):
    row = jnp.broadcast_to(log[:, None, None], (state.shape[0], 1, state.shape[2]))
    return jnp.concatenate([state, row], axis=1)


def unpack(packed):
    return packed[:, -1, 0], packed[:, :-1]


def shifted(x, axis, n):
    out = [x]
    for s in range(1, n):
        out.append(lax.ppermute(x, axis, [(j, (j + s) % n) for j in range(n)]))
    return out


def scan_pieces(logs, states, i, n):
    log_before = jnp.zeros_like(logs[0])
    before = jnp.zeros_like(states[0])
    log_after = jnp.zeros_like(logs[0])
    after = jnp.zeros_like(states[0])
    for s in range(1, n):
        early = s <= i
        weight_b = jnp.where(early, jnp.exp(log_before), 0.0)
        weight_a = jnp.where(early, 0.0, jnp.exp(log_after))
        before = before + weight_b[:, None, None] * states[s]
        after = after + weight_a[:, None, None] * states[s]
        log_before = log_before + jnp.where(early, logs[s], 0.0)
        log_after = log_after + jnp.where(early, 0.0, logs[s])
    return log_before, before, log_after, after


def exclusive_scan(log, state, axis, n):
    def shift(packed, d):
        return lax.ppermute(packed, axis, [(j, j + d) for j in range(n - d)])

    packed = pack(log, state)
    first = min(4, n - 1)
    cur_log = jnp.zeros_like(log)
    cur = jnp.zeros_like(state)
    for d in range(1, first + 1):
        got_log, got = unpack(shift(packed, d))
        cur = cur + jnp.exp(cur_log)[:, None, None] * got
        cur_log = cur_log + got_log
    d = first
    while d < n:
        got_log, got = unpack(shift(pack(cur_log, cur), d))
        cur = jnp.exp(cur_log)[:, None, None] * got + cur
        cur_log = cur_log + got_log
        d *= 2
    return cur_log, cur


def carried_state(L, S):
    rows, cols, cores = lax.axis_size("cy"), lax.axis_size("cx"), lax.axis_size("cc")
    y, x, c = lax.axis_index("cy"), lax.axis_index("cx"), lax.axis_index("cc")
    heads, size = S.shape[0], S.shape[1]
    group = heads // cores

    pair = unpack(lax.ppermute(pack(L, S), "cc", [(0, 1), (1, 0)]))
    L0 = jnp.where(c == 0, L, pair[0])
    S0 = jnp.where(c == 0, S, pair[1])
    L1 = jnp.where(c == 0, pair[0], L)
    S1 = jnp.where(c == 0, pair[1], S)
    chip_log = L0 + L1
    chip_state = jnp.exp(L1)[:, None, None] * S0 + S1
    g_log = lax.dynamic_slice_in_dim(chip_log, c * group, group, 0)
    g_state = lax.dynamic_slice_in_dim(chip_state, c * group, group, 0)

    row_pieces = [unpack(p) for p in shifted(pack(g_log, g_state), "cx", cols)]
    e_log, e_state, f_log, f_state = scan_pieces(
        [p[0] for p in row_pieces], [p[1] for p in row_pieces], x, cols
    )
    row_log = e_log + g_log + f_log
    row_state = jnp.exp(f_log)[:, None, None] * (jnp.exp(g_log)[:, None, None] * e_state + g_state) + f_state

    part = size // cols
    q_state = lax.dynamic_slice_in_dim(row_state, x * part, part, 1)
    y_log, y_state = exclusive_scan(row_log, q_state, "cy", rows)

    parts = shifted(y_state, "cx", cols)
    ordered = [lax.select_n((x - q) % cols, *parts) for q in range(cols)]
    y_full = jnp.concatenate(ordered, axis=1)

    chip_before = jnp.exp(e_log)[:, None, None] * y_full + e_state

    other = lax.ppermute(chip_before, "cc", [(0, 1), (1, 0)])
    full0 = jnp.concatenate([chip_before, other], axis=0)
    full1 = jnp.concatenate([other, chip_before], axis=0)
    chip_full = jnp.where(c == 0, full0, full1)
    return jnp.where(c == 0, chip_full, jnp.exp(L0)[:, None, None] * chip_full + S0)


def split3(x):
    hi = lax.reduce_precision(x, exponent_bits=8, mantissa_bits=7)
    rest = x - hi
    mid = lax.reduce_precision(rest, exponent_bits=8, mantissa_bits=7)
    lo = rest - mid
    return hi.astype(jnp.bfloat16), mid.astype(jnp.bfloat16), lo.astype(jnp.bfloat16)


def sum3(product, axis):
    a, b, c = jnp.split(product, 3, axis=axis)
    return (a + b) + c


def inner_head(qh, kh, vh, ch):
    count = qh.shape[0]
    target_index = jnp.arange(count)
    causal = target_index[:, None] >= target_index[None, :]
    scores = jnp.dot(qh, kh.T, preferred_element_type=F32)
    spread = jnp.where(causal, ch[:, None] - ch[None, :], 0.0)
    weights = (scores * jnp.where(causal, jnp.exp(spread), 0.0)).astype(jnp.bfloat16)
    return jnp.dot(weights, vh, preferred_element_type=F32)


def body(queries, keys, values, log_decay, gate, norm_gain):
    count, width = queries.shape
    heads = log_decay.shape[1]
    size = width // heads
    cum = jnp.cumsum(log_decay, axis=0)
    last = cum[-1]

    def cols(array, h):
        return array[:, h * size : (h + 1) * size]

    def block_state(h):
        keyed = cols(keys, h).astype(F32) * jnp.exp(last[h] - cum[:, h])[:, None]
        pieces = jnp.concatenate(split3(keyed), axis=1)
        product = lax.dot_general(pieces, cols(values, h), (((0,), (0,)), ((), ())), preferred_element_type=F32)
        return sum3(product, 0)

    state = jnp.stack([block_state(h) for h in range(heads)])

    carried = carried_state(last, state)

    joined = []
    for h in range(heads):
        qh = cols(queries, h)
        inner = inner_head(qh, cols(keys, h), cols(values, h), cum[:, h])
        across = sum3(jnp.dot(qh, jnp.concatenate(split3(carried[h]), axis=1), preferred_element_type=F32), 1)
        joined.append(inner + jnp.exp(cum[:, h])[:, None] * across)
    attended = jnp.concatenate(joined, axis=1).astype(jnp.bfloat16)

    groups = lax.axis_size("head")
    shade = attended.astype(F32)
    sums = jnp.sum(shade * shade, axis=1)
    gain = lax.dynamic_slice_in_dim(norm_gain, lax.axis_index("head") * width, width, 0)
    shaped = (shade * gain * jax.nn.sigmoid(gate.astype(F32))).astype(jnp.bfloat16)
    chunk = count // groups
    high = sums.astype(jnp.bfloat16)
    low = (sums - high.astype(F32)).astype(jnp.bfloat16)
    extra = jnp.concatenate(
        [
            high.reshape(groups, 1, chunk),
            low.reshape(groups, 1, chunk),
            jnp.zeros((groups, 1, width - 2 * chunk), jnp.bfloat16),
        ],
        axis=2,
    )
    payload = jnp.concatenate([shaped.reshape(groups, chunk, width), extra], axis=1)
    got = lax.all_to_all(payload, "head", split_axis=0, concat_axis=0, tiled=True)
    parts = got[:, -1, :].astype(F32)
    total = jnp.sum(parts[:, :chunk] + parts[:, chunk : 2 * chunk], axis=0)
    scale = lax.rsqrt(total / (width * groups) + eps_norm)
    rows_out = got[:, :chunk, :].astype(F32) * scale[None, :, None]
    return rows_out.transpose(1, 0, 2).reshape(chunk, width * groups).astype(jnp.bfloat16)


def solution(mesh):
    fine = split_ctx(mesh)
    ctx = ("cy", "cx", "cc")
    spec = P(ctx, "head")
    in_specs = (spec, spec, spec, spec, spec, P())
    out_specs = P((*ctx, "head"), None)
    return jax.shard_map(body, mesh=fine, in_specs=in_specs, out_specs=out_specs, check_vma=False)
```

```python
import jax
import jax.numpy as jnp
from jax import lax
from jax.sharding import Mesh, PartitionSpec as P

eps_norm = 1e-05
HI = lax.Precision.HIGHEST
F32 = jnp.float32


def split_ctx(mesh):
    devices = mesh.devices
    ctx_devices = list(devices[:, 0])
    rows = len({d.coords[1] for d in ctx_devices})
    cols = len({d.coords[0] for d in ctx_devices})
    cores = len(ctx_devices) // (rows * cols)
    shape = (rows, cols, cores, devices.shape[1])
    return Mesh(devices.reshape(shape), ("cy", "cx", "cc", "head"))


def pack(log, state):
    row = jnp.broadcast_to(log[:, None, None], (state.shape[0], 1, state.shape[2]))
    return jnp.concatenate([state, row], axis=1)


def unpack(packed):
    return packed[:, -1, 0], packed[:, :-1]


def shifted(x, axis, n):
    out = [x]
    for s in range(1, n):
        out.append(lax.ppermute(x, axis, [(j, (j + s) % n) for j in range(n)]))
    return out


def scan_pieces(logs, states, i, n):
    log_before = jnp.zeros_like(logs[0])
    before = jnp.zeros_like(states[0])
    log_after = jnp.zeros_like(logs[0])
    after = jnp.zeros_like(states[0])
    for s in range(1, n):
        early = s <= i
        weight_b = jnp.where(early, jnp.exp(log_before), 0.0)
        weight_a = jnp.where(early, 0.0, jnp.exp(log_after))
        before = before + weight_b[:, None, None] * states[s]
        after = after + weight_a[:, None, None] * states[s]
        log_before = log_before + jnp.where(early, logs[s], 0.0)
        log_after = log_after + jnp.where(early, 0.0, logs[s])
    return log_before, before, log_after, after


def exclusive_scan(log, state, axis, n):
    def shift(packed, d):
        return lax.ppermute(packed, axis, [(j, j + d) for j in range(n - d)])

    packed = pack(log, state)
    first = min(4, n - 1)
    cur_log = jnp.zeros_like(log)
    cur = jnp.zeros_like(state)
    for d in range(1, first + 1):
        got_log, got = unpack(shift(packed, d))
        cur = cur + jnp.exp(cur_log)[:, None, None] * got
        cur_log = cur_log + got_log
    d = first
    while d < n:
        got_log, got = unpack(shift(pack(cur_log, cur), d))
        cur = jnp.exp(cur_log)[:, None, None] * got + cur
        cur_log = cur_log + got_log
        d *= 2
    return cur_log, cur


def exclusive_scan_rounds(log, state, axis, n, widths):
    def shift(packed, d):
        return lax.ppermute(packed, axis, [(j, j + d) for j in range(n - d)])

    cur_log, cur = jnp.zeros_like(log), jnp.zeros_like(state)
    sent, window = pack(log, state), 1
    for count in widths:
        for j in range(1, count + 1) if window == 1 else range(1, count):
            d = j * window
            if d >= n:
                break
            got_log, got = unpack(shift(sent, d))
            cur = cur + jnp.exp(cur_log)[:, None, None] * got
            cur_log = cur_log + got_log
        window = window * count
        sent = pack(cur_log, cur)
    return cur_log, cur


def carried_state(L, S):
    rows, cols, cores = lax.axis_size("cy"), lax.axis_size("cx"), lax.axis_size("cc")
    y, x, c = lax.axis_index("cy"), lax.axis_index("cx"), lax.axis_index("cc")
    heads, size = S.shape[0], S.shape[1]
    group = heads // cores

    pair = unpack(lax.ppermute(pack(L, S), "cc", [(0, 1), (1, 0)]))
    L0 = jnp.where(c == 0, L, pair[0])
    S0 = jnp.where(c == 0, S, pair[1])
    L1 = jnp.where(c == 0, pair[0], L)
    S1 = jnp.where(c == 0, pair[1], S)
    chip_log = L0 + L1
    chip_state = jnp.exp(L1)[:, None, None] * S0 + S1
    g_log = lax.dynamic_slice_in_dim(chip_log, c * group, group, 0)
    g_state = lax.dynamic_slice_in_dim(chip_state, c * group, group, 0)

    chips = rows * cols
    e_log, chip_before = exclusive_scan_rounds(g_log, g_state, ("cy", "cx"), chips, (4, 4, 2))

    other = lax.ppermute(chip_before, "cc", [(0, 1), (1, 0)])
    full0 = jnp.concatenate([chip_before, other], axis=0)
    full1 = jnp.concatenate([other, chip_before], axis=0)
    chip_full = jnp.where(c == 0, full0, full1)
    return jnp.where(c == 0, chip_full, jnp.exp(L0)[:, None, None] * chip_full + S0)


def inner_head(qh, kh, vh, ch):
    count = qh.shape[0]
    target_index = jnp.arange(count)
    causal = target_index[:, None] >= target_index[None, :]
    scores = jnp.dot(qh, kh.T, preferred_element_type=F32)
    spread = jnp.where(causal, ch[:, None] - ch[None, :], 0.0)
    weights = (scores * jnp.where(causal, jnp.exp(spread), 0.0)).astype(jnp.bfloat16)
    return jnp.dot(weights, vh, preferred_element_type=F32)


def body(queries, keys, values, log_decay, gate, norm_gain):
    count, width = queries.shape
    heads = log_decay.shape[1]
    size = width // heads
    cum = jnp.cumsum(log_decay, axis=0)
    last = cum[-1]

    def cols(array, h):
        return array[:, h * size : (h + 1) * size]

    state = jnp.stack(
        [
            jnp.dot(
                (cols(keys, h).astype(F32) * jnp.exp(last[h] - cum[:, h])[:, None]).T,
                cols(values, h).astype(F32),
                precision=HI,
            )
            for h in range(heads)
        ]
    )

    carried = carried_state(last, state)

    joined = []
    for h in range(heads):
        qh = cols(queries, h)
        inner = inner_head(qh, cols(keys, h), cols(values, h), cum[:, h])
        across = jnp.dot(qh.astype(F32), carried[h], precision=HI)
        joined.append(inner + jnp.exp(cum[:, h])[:, None] * across)
    attended = jnp.concatenate(joined, axis=1).astype(jnp.bfloat16)

    groups = lax.axis_size("head")
    shade = attended.astype(F32)
    sums = jnp.sum(shade * shade, axis=1)
    gain = lax.dynamic_slice_in_dim(norm_gain, lax.axis_index("head") * width, width, 0)
    shaped = (shade * gain * jax.nn.sigmoid(gate.astype(F32))).astype(jnp.bfloat16)
    chunk = count // groups
    high = sums.astype(jnp.bfloat16)
    low = (sums - high.astype(F32)).astype(jnp.bfloat16)
    extra = jnp.concatenate(
        [
            high.reshape(groups, 1, chunk),
            low.reshape(groups, 1, chunk),
            jnp.zeros((groups, 1, width - 2 * chunk), jnp.bfloat16),
        ],
        axis=2,
    )
    payload = jnp.concatenate([shaped.reshape(groups, chunk, width), extra], axis=1)
    got = lax.all_to_all(payload, "head", split_axis=0, concat_axis=0, tiled=True)
    parts = got[:, -1, :].astype(F32)
    total = jnp.sum(parts[:, :chunk] + parts[:, chunk : 2 * chunk], axis=0)
    scale = lax.rsqrt(total / (width * groups) + eps_norm)
    rows_out = got[:, :chunk, :].astype(F32) * scale[None, :, None]
    return rows_out.transpose(1, 0, 2).reshape(chunk, width * groups).astype(jnp.bfloat16)


def solution(mesh):
    fine = split_ctx(mesh)
    ctx = ("cy", "cx", "cc")
    spec = P(ctx, "head")
    in_specs = (spec, spec, spec, spec, spec, P())
    out_specs = P((*ctx, "head"), None)
    return jax.shard_map(body, mesh=fine, in_specs=in_specs, out_specs=out_specs, check_vma=False)
```

```python
import jax
import jax.numpy as jnp
from jax import lax
from jax.sharding import Mesh, PartitionSpec as P

eps_norm = 1e-05
HI = lax.Precision.HIGHEST
F32 = jnp.float32


def split_ctx(mesh):
    devices = mesh.devices
    ctx_devices = list(devices[:, 0])
    rows = len({d.coords[1] for d in ctx_devices})
    cols = len({d.coords[0] for d in ctx_devices})
    cores = len(ctx_devices) // (rows * cols)
    shape = (rows, cols, cores, devices.shape[1])
    return Mesh(devices.reshape(shape), ("cy", "cx", "cc", "head"))


def pack(log, state):
    row = jnp.broadcast_to(log[:, None, None], (state.shape[0], 1, state.shape[2]))
    return jnp.concatenate([state, row], axis=1)


def unpack(packed):
    return packed[:, -1, 0], packed[:, :-1]


def shifted(x, axis, n):
    out = [x]
    for s in range(1, n):
        out.append(lax.ppermute(x, axis, [(j, (j + s) % n) for j in range(n)]))
    return out


def scan_pieces(logs, states, i, n):
    log_before = jnp.zeros_like(logs[0])
    before = jnp.zeros_like(states[0])
    log_after = jnp.zeros_like(logs[0])
    after = jnp.zeros_like(states[0])
    for s in range(1, n):
        early = s <= i
        weight_b = jnp.where(early, jnp.exp(log_before), 0.0)
        weight_a = jnp.where(early, 0.0, jnp.exp(log_after))
        before = before + weight_b[:, None, None] * states[s]
        after = after + weight_a[:, None, None] * states[s]
        log_before = log_before + jnp.where(early, logs[s], 0.0)
        log_after = log_after + jnp.where(early, 0.0, logs[s])
    return log_before, before, log_after, after


def exclusive_scan(log, state, axis, n):
    def shift(packed, d):
        return lax.ppermute(packed, axis, [(j, j + d) for j in range(n - d)])

    packed = pack(log, state)
    first = min(4, n - 1)
    cur_log = jnp.zeros_like(log)
    cur = jnp.zeros_like(state)
    for d in range(1, first + 1):
        got_log, got = unpack(shift(packed, d))
        cur = cur + jnp.exp(cur_log)[:, None, None] * got
        cur_log = cur_log + got_log
    d = first
    while d < n:
        got_log, got = unpack(shift(pack(cur_log, cur), d))
        cur = jnp.exp(cur_log)[:, None, None] * got + cur
        cur_log = cur_log + got_log
        d *= 2
    return cur_log, cur


def carried_state(L, S):
    rows, cols, cores = lax.axis_size("cy"), lax.axis_size("cx"), lax.axis_size("cc")
    y, x, c = lax.axis_index("cy"), lax.axis_index("cx"), lax.axis_index("cc")
    heads, size = S.shape[0], S.shape[1]
    group = heads // cores

    pair = unpack(lax.ppermute(pack(L, S), "cc", [(0, 1), (1, 0)]))
    L0 = jnp.where(c == 0, L, pair[0])
    S0 = jnp.where(c == 0, S, pair[1])
    L1 = jnp.where(c == 0, pair[0], L)
    S1 = jnp.where(c == 0, pair[1], S)
    chip_log = L0 + L1
    chip_state = jnp.exp(L1)[:, None, None] * S0 + S1
    g_log = lax.dynamic_slice_in_dim(chip_log, c * group, group, 0)
    g_state = lax.dynamic_slice_in_dim(chip_state, c * group, group, 0)

    row_pieces = [unpack(p) for p in shifted(pack(g_log, g_state), "cx", cols)]
    e_log, e_state, f_log, f_state = scan_pieces(
        [p[0] for p in row_pieces], [p[1] for p in row_pieces], x, cols
    )
    row_log = e_log + g_log + f_log
    row_state = jnp.exp(f_log)[:, None, None] * (jnp.exp(g_log)[:, None, None] * e_state + g_state) + f_state

    part = size // cols
    q_state = lax.dynamic_slice_in_dim(row_state, x * part, part, 1)
    y_log, y_state = exclusive_scan(row_log, q_state, "cy", rows)

    parts = shifted(y_state, "cx", cols)
    ordered = [lax.select_n((x - q) % cols, *parts) for q in range(cols)]
    y_full = jnp.concatenate(ordered, axis=1)

    chip_before = jnp.exp(e_log)[:, None, None] * y_full + e_state

    other = lax.ppermute(chip_before, "cc", [(0, 1), (1, 0)])
    full0 = jnp.concatenate([chip_before, other], axis=0)
    full1 = jnp.concatenate([other, chip_before], axis=0)
    chip_full = jnp.where(c == 0, full0, full1)
    return jnp.where(c == 0, chip_full, jnp.exp(L0)[:, None, None] * chip_full + S0)


def split3(x):
    hi = lax.reduce_precision(x, exponent_bits=8, mantissa_bits=7)
    rest = x - hi
    mid = lax.reduce_precision(rest, exponent_bits=8, mantissa_bits=7)
    lo = rest - mid
    return hi.astype(jnp.bfloat16), mid.astype(jnp.bfloat16), lo.astype(jnp.bfloat16)


def sum3(product, axis):
    a, b, c = jnp.split(product, 3, axis=axis)
    return (a + b) + c


def inner_head(qh, kh, vh, ch):
    count = qh.shape[0]
    target_index = jnp.arange(count)
    causal = target_index[:, None] >= target_index[None, :]
    scores = jnp.dot(qh, kh.T, preferred_element_type=F32)
    spread = jnp.where(causal, ch[:, None] - ch[None, :], 0.0)
    weights = (scores * jnp.where(causal, jnp.exp(spread), 0.0)).astype(jnp.bfloat16)
    return jnp.dot(weights, vh, preferred_element_type=F32)


def body(queries, keys, values, log_decay, gate, norm_gain):
    count, width = queries.shape
    heads = log_decay.shape[1]
    size = width // heads
    cum = jnp.cumsum(log_decay, axis=0)
    last = cum[-1]

    def cols(array, h):
        return array[:, h * size : (h + 1) * size]

    def block_state(h):
        keyed = cols(keys, h).astype(F32) * jnp.exp(last[h] - cum[:, h])[:, None]
        pieces = jnp.concatenate(split3(keyed), axis=1)
        product = lax.dot_general(pieces, cols(values, h), (((0,), (0,)), ((), ())), preferred_element_type=F32)
        return sum3(product, 0)

    state = jnp.stack([block_state(h) for h in range(heads)])

    carried = carried_state(last, state)

    joined = []
    for h in range(heads):
        qh = cols(queries, h)
        inner = inner_head(qh, cols(keys, h), cols(values, h), cum[:, h])
        across = jnp.dot(qh.astype(F32), carried[h], precision=HI)
        joined.append(inner + jnp.exp(cum[:, h])[:, None] * across)
    attended = jnp.concatenate(joined, axis=1).astype(jnp.bfloat16)

    groups = lax.axis_size("head")
    shade = attended.astype(F32)
    sums = jnp.sum(shade * shade, axis=1)
    gain = lax.dynamic_slice_in_dim(norm_gain, lax.axis_index("head") * width, width, 0)
    shaped = (shade * gain * jax.nn.sigmoid(gate.astype(F32))).astype(jnp.bfloat16)
    chunk = count // groups
    high = sums.astype(jnp.bfloat16)
    low = (sums - high.astype(F32)).astype(jnp.bfloat16)
    extra = jnp.concatenate(
        [
            high.reshape(groups, 1, chunk),
            low.reshape(groups, 1, chunk),
            jnp.zeros((groups, 1, width - 2 * chunk), jnp.bfloat16),
        ],
        axis=2,
    )
    payload = jnp.concatenate([shaped.reshape(groups, chunk, width), extra], axis=1)
    got = lax.all_to_all(payload, "head", split_axis=0, concat_axis=0, tiled=True)
    parts = got[:, -1, :].astype(F32)
    total = jnp.sum(parts[:, :chunk] + parts[:, chunk : 2 * chunk], axis=0)
    scale = lax.rsqrt(total / (width * groups) + eps_norm)
    rows_out = got[:, :chunk, :].astype(F32) * scale[None, :, None]
    return rows_out.transpose(1, 0, 2).reshape(chunk, width * groups).astype(jnp.bfloat16)


def solution(mesh):
    fine = split_ctx(mesh)
    ctx = ("cy", "cx", "cc")
    spec = P(ctx, "head")
    in_specs = (spec, spec, spec, spec, spec, P())
    out_specs = P((*ctx, "head"), None)
    return jax.shard_map(body, mesh=fine, in_specs=in_specs, out_specs=out_specs, check_vma=False)
```

```python
import jax
import jax.numpy as jnp
from jax import lax
from jax.sharding import Mesh, PartitionSpec as P

eps_norm = 1e-05
HI = lax.Precision.HIGHEST
F32 = jnp.float32


def split_ctx(mesh):
    devices = mesh.devices
    ctx_devices = list(devices[:, 0])
    rows = len({d.coords[1] for d in ctx_devices})
    cols = len({d.coords[0] for d in ctx_devices})
    cores = len(ctx_devices) // (rows * cols)
    shape = (rows, cols, cores, devices.shape[1])
    return Mesh(devices.reshape(shape), ("cy", "cx", "cc", "head"))


def pack(log, state):
    row = jnp.broadcast_to(log[:, None, None], (state.shape[0], 1, state.shape[2]))
    return jnp.concatenate([state, row], axis=1)


def unpack(packed):
    return packed[:, -1, 0], packed[:, :-1]


def shifted(x, axis, n):
    out = [x]
    for s in range(1, n):
        out.append(lax.ppermute(x, axis, [(j, (j + s) % n) for j in range(n)]))
    return out


def scan_pieces(logs, states, i, n):
    log_before = jnp.zeros_like(logs[0])
    before = jnp.zeros_like(states[0])
    log_after = jnp.zeros_like(logs[0])
    after = jnp.zeros_like(states[0])
    for s in range(1, n):
        early = s <= i
        weight_b = jnp.where(early, jnp.exp(log_before), 0.0)
        weight_a = jnp.where(early, 0.0, jnp.exp(log_after))
        before = before + weight_b[:, None, None] * states[s]
        after = after + weight_a[:, None, None] * states[s]
        log_before = log_before + jnp.where(early, logs[s], 0.0)
        log_after = log_after + jnp.where(early, 0.0, logs[s])
    return log_before, before, log_after, after


def exclusive_scan(log, state, axis, n):
    def shift(packed, d):
        return lax.ppermute(packed, axis, [(j, j + d) for j in range(n - d)])

    packed = pack(log, state)
    first = min(4, n - 1)
    cur_log = jnp.zeros_like(log)
    cur = jnp.zeros_like(state)
    for d in range(1, first + 1):
        got_log, got = unpack(shift(packed, d))
        cur = cur + jnp.exp(cur_log)[:, None, None] * got
        cur_log = cur_log + got_log
    d = first
    while d < n:
        got_log, got = unpack(shift(pack(cur_log, cur), d))
        cur = jnp.exp(cur_log)[:, None, None] * got + cur
        cur_log = cur_log + got_log
        d *= 2
    return cur_log, cur


def carried_state(L, S):
    rows, cols, cores = lax.axis_size("cy"), lax.axis_size("cx"), lax.axis_size("cc")
    y, x, c = lax.axis_index("cy"), lax.axis_index("cx"), lax.axis_index("cc")
    heads, size = S.shape[0], S.shape[1]
    group = heads // cores

    line = cols * cores
    i = x * cores + c

    def group_of(g):
        return (
            lax.dynamic_slice_in_dim(L, g * group, group, 0),
            lax.dynamic_slice_in_dim(S, g * group, group, 0),
        )

    own_log, own = group_of(c)
    logs, states = [own_log], [own]
    for s in range(1, line):
        sent = pack(*group_of((c + s) % cores))
        got_log, got = unpack(lax.ppermute(sent, ("cx", "cc"), [(j, (j + s) % line) for j in range(line)]))
        logs.append(got_log)
        states.append(got)
    e_log, e_state, f_log, f_state = scan_pieces(logs, states, i, line)
    c_log = jnp.zeros_like(own_log)
    c_state = jnp.zeros_like(own)
    for s in range(1, line):
        early = jnp.logical_and(s <= i, s > c)
        c_state = c_state + jnp.where(early, jnp.exp(c_log), 0.0)[:, None, None] * states[s]
        c_log = c_log + jnp.where(early, logs[s], 0.0)
    row_log = e_log + own_log + f_log
    row_state = jnp.exp(f_log)[:, None, None] * (jnp.exp(own_log)[:, None, None] * e_state + own) + f_state

    part = size // cols
    q_state = lax.dynamic_slice_in_dim(row_state, x * part, part, 1)
    y_log, y_state = exclusive_scan(row_log, q_state, "cy", rows)

    parts = shifted(y_state, "cx", cols)
    ordered = [lax.select_n((x - q) % cols, *parts) for q in range(cols)]
    y_full = jnp.concatenate(ordered, axis=1)

    mine = jnp.exp(e_log)[:, None, None] * y_full + e_state
    chip_before = jnp.exp(c_log)[:, None, None] * y_full + c_state
    first_log, first = group_of(0)
    sent = jnp.where(c == 0, jnp.exp(first_log)[:, None, None] * mine + first, chip_before)
    other = lax.ppermute(sent, "cc", [(0, 1), (1, 0)])
    full0 = jnp.concatenate([mine, other], axis=0)
    full1 = jnp.concatenate([other, mine], axis=0)
    return jnp.where(c == 0, full0, full1)


def inner_head(qh, kh, vh, ch):
    count = qh.shape[0]
    target_index = jnp.arange(count)
    causal = target_index[:, None] >= target_index[None, :]
    scores = jnp.dot(qh, kh.T, preferred_element_type=F32)
    spread = jnp.where(causal, ch[:, None] - ch[None, :], 0.0)
    weights = (scores * jnp.where(causal, jnp.exp(spread), 0.0)).astype(jnp.bfloat16)
    return jnp.dot(weights, vh, preferred_element_type=F32)


def body(queries, keys, values, log_decay, gate, norm_gain):
    count, width = queries.shape
    heads = log_decay.shape[1]
    size = width // heads
    cum = jnp.cumsum(log_decay, axis=0)
    last = cum[-1]

    def cols(array, h):
        return array[:, h * size : (h + 1) * size]

    state = jnp.stack(
        [
            jnp.dot(
                (cols(keys, h).astype(F32) * jnp.exp(last[h] - cum[:, h])[:, None]).T,
                cols(values, h).astype(F32),
                precision=HI,
            )
            for h in range(heads)
        ]
    )

    carried = carried_state(last, state)

    joined = []
    for h in range(heads):
        qh = cols(queries, h)
        inner = inner_head(qh, cols(keys, h), cols(values, h), cum[:, h])
        across = jnp.dot(qh.astype(F32), carried[h], precision=HI)
        joined.append(inner + jnp.exp(cum[:, h])[:, None] * across)
    attended = jnp.concatenate(joined, axis=1).astype(jnp.bfloat16)

    groups = lax.axis_size("head")
    shade = attended.astype(F32)
    sums = jnp.sum(shade * shade, axis=1)
    gain = lax.dynamic_slice_in_dim(norm_gain, lax.axis_index("head") * width, width, 0)
    shaped = (shade * gain * jax.nn.sigmoid(gate.astype(F32))).astype(jnp.bfloat16)
    chunk = count // groups
    high = sums.astype(jnp.bfloat16)
    low = (sums - high.astype(F32)).astype(jnp.bfloat16)
    extra = jnp.concatenate(
        [
            high.reshape(groups, 1, chunk),
            low.reshape(groups, 1, chunk),
            jnp.zeros((groups, 1, width - 2 * chunk), jnp.bfloat16),
        ],
        axis=2,
    )
    payload = jnp.concatenate([shaped.reshape(groups, chunk, width), extra], axis=1)
    got = lax.all_to_all(payload, "head", split_axis=0, concat_axis=0, tiled=True)
    parts = got[:, -1, :].astype(F32)
    total = jnp.sum(parts[:, :chunk] + parts[:, chunk : 2 * chunk], axis=0)
    scale = lax.rsqrt(total / (width * groups) + eps_norm)
    rows_out = got[:, :chunk, :].astype(F32) * scale[None, :, None]
    return rows_out.transpose(1, 0, 2).reshape(chunk, width * groups).astype(jnp.bfloat16)


def solution(mesh):
    fine = split_ctx(mesh)
    ctx = ("cy", "cx", "cc")
    spec = P(ctx, "head")
    in_specs = (spec, spec, spec, spec, spec, P())
    out_specs = P((*ctx, "head"), None)
    return jax.shard_map(body, mesh=fine, in_specs=in_specs, out_specs=out_specs, check_vma=False)
```

```python
import jax
import jax.numpy as jnp
from jax import lax
from jax.sharding import Mesh, PartitionSpec as P

eps_norm = 1e-05
HI = lax.Precision.HIGHEST
F32 = jnp.float32


def split_ctx(mesh):
    devices = mesh.devices
    ctx_devices = list(devices[:, 0])
    rows = len({d.coords[1] for d in ctx_devices})
    cols = len({d.coords[0] for d in ctx_devices})
    cores = len(ctx_devices) // (rows * cols)
    shape = (rows, cols, cores, devices.shape[1])
    return Mesh(devices.reshape(shape), ("cy", "cx", "cc", "head"))


def pack(log, state):
    row = jnp.broadcast_to(log[:, None, None], (state.shape[0], 1, state.shape[2]))
    return jnp.concatenate([state, row], axis=1)


def unpack(packed):
    return packed[:, -1, 0], packed[:, :-1]


def shifted(x, axis, n):
    out = [x]
    for s in range(1, n):
        out.append(lax.ppermute(x, axis, [(j, (j + s) % n) for j in range(n)]))
    return out


def scan_pieces(logs, states, i, n):
    log_before = jnp.zeros_like(logs[0])
    before = jnp.zeros_like(states[0])
    log_after = jnp.zeros_like(logs[0])
    after = jnp.zeros_like(states[0])
    for s in range(1, n):
        early = s <= i
        weight_b = jnp.where(early, jnp.exp(log_before), 0.0)
        weight_a = jnp.where(early, 0.0, jnp.exp(log_after))
        before = before + weight_b[:, None, None] * states[s]
        after = after + weight_a[:, None, None] * states[s]
        log_before = log_before + jnp.where(early, logs[s], 0.0)
        log_after = log_after + jnp.where(early, 0.0, logs[s])
    return log_before, before, log_after, after


def exclusive_scan(log, state, axis, n):
    def shift(packed, d):
        return lax.ppermute(packed, axis, [(j, j + d) for j in range(n - d)])

    packed = pack(log, state)
    first = n - 1
    cur_log = jnp.zeros_like(log)
    cur = jnp.zeros_like(state)
    for d in range(1, first + 1):
        got_log, got = unpack(shift(packed, d))
        cur = cur + jnp.exp(cur_log)[:, None, None] * got
        cur_log = cur_log + got_log
    d = first
    while d < n - 1:
        got_log, got = unpack(shift(pack(cur_log, cur), d))
        cur = jnp.exp(cur_log)[:, None, None] * got + cur
        cur_log = cur_log + got_log
        d *= 2
    return cur_log, cur


def carried_state(L, S):
    rows, cols, cores = lax.axis_size("cy"), lax.axis_size("cx"), lax.axis_size("cc")
    y, x, c = lax.axis_index("cy"), lax.axis_index("cx"), lax.axis_index("cc")
    heads, size = S.shape[0], S.shape[1]
    group = heads // cores

    pair = unpack(lax.ppermute(pack(L, S), "cc", [(0, 1), (1, 0)]))
    L0 = jnp.where(c == 0, L, pair[0])
    S0 = jnp.where(c == 0, S, pair[1])
    L1 = jnp.where(c == 0, pair[0], L)
    S1 = jnp.where(c == 0, pair[1], S)
    chip_log = L0 + L1
    chip_state = jnp.exp(L1)[:, None, None] * S0 + S1
    g_log = lax.dynamic_slice_in_dim(chip_log, c * group, group, 0)
    g_state = lax.dynamic_slice_in_dim(chip_state, c * group, group, 0)

    row_pieces = [unpack(p) for p in shifted(pack(g_log, g_state), "cx", cols)]
    e_log, e_state, f_log, f_state = scan_pieces(
        [p[0] for p in row_pieces], [p[1] for p in row_pieces], x, cols
    )
    row_log = e_log + g_log + f_log
    row_state = jnp.exp(f_log)[:, None, None] * (jnp.exp(g_log)[:, None, None] * e_state + g_state) + f_state

    part = size // cols
    q_state = lax.dynamic_slice_in_dim(row_state, x * part, part, 1)
    y_log, y_state = exclusive_scan(row_log, q_state, "cy", rows)

    parts = shifted(y_state, "cx", cols)
    ordered = [lax.select_n((x - q) % cols, *parts) for q in range(cols)]
    y_full = jnp.concatenate(ordered, axis=1)

    chip_before = jnp.exp(e_log)[:, None, None] * y_full + e_state

    other = lax.ppermute(chip_before, "cc", [(0, 1), (1, 0)])
    full0 = jnp.concatenate([chip_before, other], axis=0)
    full1 = jnp.concatenate([other, chip_before], axis=0)
    chip_full = jnp.where(c == 0, full0, full1)
    return jnp.where(c == 0, chip_full, jnp.exp(L0)[:, None, None] * chip_full + S0)


def inner_head(qh, kh, vh, ch):
    count = qh.shape[0]
    target_index = jnp.arange(count)
    causal = target_index[:, None] >= target_index[None, :]
    scores = jnp.dot(qh, kh.T, preferred_element_type=F32)
    spread = jnp.where(causal, ch[:, None] - ch[None, :], 0.0)
    weights = (scores * jnp.where(causal, jnp.exp(spread), 0.0)).astype(jnp.bfloat16)
    return jnp.dot(weights, vh, preferred_element_type=F32)


def body(queries, keys, values, log_decay, gate, norm_gain):
    count, width = queries.shape
    heads = log_decay.shape[1]
    size = width // heads
    cum = jnp.cumsum(log_decay, axis=0)
    last = cum[-1]

    def cols(array, h):
        return array[:, h * size : (h + 1) * size]

    state = jnp.stack(
        [
            jnp.dot(
                (cols(keys, h).astype(F32) * jnp.exp(last[h] - cum[:, h])[:, None]).T,
                cols(values, h).astype(F32),
                precision=HI,
            )
            for h in range(heads)
        ]
    )

    carried = carried_state(last, state)

    joined = []
    for h in range(heads):
        qh = cols(queries, h)
        inner = inner_head(qh, cols(keys, h), cols(values, h), cum[:, h])
        across = jnp.dot(qh.astype(F32), carried[h], precision=HI)
        joined.append(inner + jnp.exp(cum[:, h])[:, None] * across)
    attended = jnp.concatenate(joined, axis=1).astype(jnp.bfloat16)

    groups = lax.axis_size("head")
    shade = attended.astype(F32)
    sums = jnp.sum(shade * shade, axis=1)
    gain = lax.dynamic_slice_in_dim(norm_gain, lax.axis_index("head") * width, width, 0)
    shaped = (shade * gain * jax.nn.sigmoid(gate.astype(F32))).astype(jnp.bfloat16)
    chunk = count // groups
    high = sums.astype(jnp.bfloat16)
    low = (sums - high.astype(F32)).astype(jnp.bfloat16)
    extra = jnp.concatenate(
        [
            high.reshape(groups, 1, chunk),
            low.reshape(groups, 1, chunk),
            jnp.zeros((groups, 1, width - 2 * chunk), jnp.bfloat16),
        ],
        axis=2,
    )
    payload = jnp.concatenate([shaped.reshape(groups, chunk, width), extra], axis=1)
    got = lax.all_to_all(payload, "head", split_axis=0, concat_axis=0, tiled=True)
    parts = got[:, -1, :].astype(F32)
    total = jnp.sum(parts[:, :chunk] + parts[:, chunk : 2 * chunk], axis=0)
    scale = lax.rsqrt(total / (width * groups) + eps_norm)
    rows_out = got[:, :chunk, :].astype(F32) * scale[None, :, None]
    return rows_out.transpose(1, 0, 2).reshape(chunk, width * groups).astype(jnp.bfloat16)


def solution(mesh):
    fine = split_ctx(mesh)
    ctx = ("cy", "cx", "cc")
    spec = P(ctx, "head")
    in_specs = (spec, spec, spec, spec, spec, P())
    out_specs = P((*ctx, "head"), None)
    return jax.shard_map(body, mesh=fine, in_specs=in_specs, out_specs=out_specs, check_vma=False)
```
